32 devices in a mesh: dom: 8 (over z, y), band: 4 (over x, core).
Axes of the slice: x: 2, y: 2, z: 4, core: 2. Of those that a mesh axis runs over, the one named last changes fastest.
Arguments:
- wavefunctions: float32 [3072, 1024], P('dom', 'band'), may hold values from -6 to 6
- cell_matrix: float32 [16, 512, 512], P('dom'), may hold values from -0.25 to 0.25
- connectivity: int32 [16, 512], P('dom'), may hold values from 0 to 639, as said below
- projector: float32 [32, 16, 512], P('dom', None, 'band'), may hold values from -0.25 to 0.25
- coupling: float32 [32, 16], P('dom'), may hold values from 0.5 to 4
- atom_start: int32 [32], P('dom'), may hold values from 0 to 128
- atom_count: int32 [8], P('dom'), may hold values from 1 to 4, as said below
Outputs:
- filtered: float32 [3072, 1024], P('dom', 'band')
The draws below stay inside these ranges and needn't reach their ends.
Inputs may be any that keep to these rules, and one draw needn't show every extreme that they name: `connectivity`: row c holds 512 distinct rows of its partition's extended block (the 128 rows before the partition's own, its 384 own rows, the 128 rows after), all within 0 to 639, both ends included. `atom_count`: at least one partition has all 4 slots live.
All inputs are finite; a program needn't handle non-finite values.
Results may differ from the reference program's by a relative error of at most 0.0003.
Values sent between devices are 32-bit elements; how exact they have to be, the bound alone decides.
No kernel may reach another device: no remote copies, remote signals or barrier semaphores. Data moves between devices by JAX's collectives and lax.ppermute only.
A program may use at most 64 MiB of HBM per device.

```python
import math
import jax
import jax.numpy as jnp
from jax import lax

NODES = 512
NPROJ = 16
SUPPORT = 512
GHOST = 128
CELLS = 2
SLOTS = 4
OWN = 384
EXT = 640
WIN = 640
STRIDE = 0
PARTS_SIZE = 8
TOTAL = 3072
NBANDS = 1024
NCELLS = 16
NATOMS = 32


def draw_connectivity(key, part):
    cell_keys = jax.random.split(jax.random.fold_in(key, 7), NCELLS)

    def one_cell(cell_key):
        inner_nodes = jax.random.permutation(cell_key, WIN - 2)[:NODES - 2] + 1
        ends = jnp.array([0, WIN - 1], jnp.int32)
        return jnp.concatenate([ends, inner_nodes.astype(jnp.int32)])
    picked = jax.vmap(one_cell)(cell_keys)
    offsets = jnp.arange(NCELLS, dtype=jnp.int32) % CELLS * STRIDE
    return (picked + offsets[:, None]).astype(jnp.int32)


def draw_atom_count(key, part):
    base_key = jax.random.fold_in(key, 11)
    heavy_key = jax.random.fold_in(key, 12)
    light_counts = jax.random.randint(base_key, (PARTS_SIZE,), 1, 3)
    rank_order = jax.random.permutation(heavy_key, PARTS_SIZE)
    return jnp.where(rank_order < max(1, PARTS_SIZE // 8), SLOTS, light_counts).astype(jnp.int32)


def place_ends(values, key, smallest, top_value):
    extent = values.shape
    index_at = [jax.random.randint(jax.random.fold_in(key, axis), (), 0, extent[axis]) for axis in range(len(extent))]
    values = values.at[tuple(index_at)].set(smallest)
    longest = extent.index(max(extent))
    index_at[longest] = (index_at[longest] + 1) % extent[longest]
    return values.at[tuple(index_at)].set(top_value)


def block_levels(key, dims, pieces, least, top_value):
    def one(axis_at, parts):
        heights = jax.random.uniform(jax.random.fold_in(jax.random.fold_in(key, 6), axis_at), (parts,), jnp.float32, least / len(pieces), top_value / len(pieces))
        return jnp.repeat(jnp.exp(heights), dims[axis_at] // parts).reshape((-1,) + (1,) * (len(dims) - axis_at - 1))

    loudness = one(*pieces[0])
    for cut in pieces[1:]:
        loudness = loudness * one(*cut)
    return loudness


def bell_draw(key, shape, spread, bound, shards=(), kind=jnp.bfloat16):
    values = jax.random.normal(key, shape, jnp.float32) * spread
    if len(shards) > 0:
        values = block_levels(key, shape, shards, -0.22, 0.18) * values
    return jnp.clip(values, min=-bound, max=bound).astype(kind)


def setup_inputs(seed: int = 0) -> dict:
    key_list = jax.random.split(jax.random.key(seed), 8)
    return {
        "wavefunctions": bell_draw(key_list[0], (TOTAL, NBANDS), 1.0, 6.0, ((0, 8), (1, 4)), jnp.float32),
        "cell_matrix": bell_draw(key_list[1], (NCELLS, NODES, NODES), NODES ** -0.5, 0.25, ((0, 8),), jnp.float32),
        "connectivity": draw_connectivity(jax.random.fold_in(key_list[7], 71), 0),
        "projector": bell_draw(key_list[3], (NATOMS, NPROJ, SUPPORT), SUPPORT ** -0.5, 0.25, ((0, 8), (2, 4)), jnp.float32),
        "coupling": jnp.clip(jnp.exp(math.log(4.0) - 2.0794415 * jax.random.uniform(key_list[4], (NATOMS, NPROJ), jnp.float32) ** block_levels(key_list[4], (NATOMS, NPROJ), ((0, 8),), -0.2, 0.2)), 0.5, 4.0),
        "atom_start": place_ends(jax.random.randint(key_list[5], (NATOMS,), 0, EXT - SUPPORT + 1), jax.random.fold_in(key_list[5], 1), 0, EXT - SUPPORT).astype(jnp.int32),
        "atom_count": draw_atom_count(jax.random.fold_in(key_list[7], 71), 0),
    }


filter_center = 0.25
filter_half = 2.0
highest = lax.Precision.HIGHEST


def partition_apply(extended, matrices, node_map, atom_proj, atom_coupling, starts, live_count):
    contributions = jnp.zeros(extended.shape, jnp.float32)
    for cell_index in range(CELLS):
        node_ids = node_map[cell_index]
        gathered = jnp.take(extended, node_ids, axis=0)
        result = jnp.dot(matrices[cell_index], gathered, precision=highest, preferred_element_type=jnp.float32)
        contributions = contributions.at[node_ids].add(result)
    for slot_index in range(SLOTS):
        first_row = starts[slot_index]
        window = lax.dynamic_slice_in_dim(extended, first_row, SUPPORT, 0)
        coefficients = jnp.dot(atom_proj[slot_index], window, precision=highest, preferred_element_type=jnp.float32)
        live = (slot_index < live_count).astype(jnp.float32)
        scaled = coefficients * (atom_coupling[slot_index] * live)[:, None]
        update = jnp.dot(atom_proj[slot_index].T, scaled, precision=highest, preferred_element_type=jnp.float32)
        current = lax.dynamic_slice_in_dim(contributions, first_row, SUPPORT, 0)
        contributions = lax.dynamic_update_slice_in_dim(contributions, current + update, first_row, 0)
    return contributions


def hamiltonian(vectors, cell_matrix, connectivity, projector, coupling, atom_start, atom_count):
    blocks = vectors.reshape(PARTS_SIZE, OWN, NBANDS)
    zero_block = jnp.zeros((1, GHOST, NBANDS), jnp.float32)
    before = jnp.concatenate([zero_block, blocks[:-1, OWN - GHOST:]], axis=0)
    after = jnp.concatenate([blocks[1:, :GHOST], zero_block], axis=0)
    matrices = cell_matrix.reshape(PARTS_SIZE, CELLS, NODES, NODES)
    node_map = connectivity.reshape(PARTS_SIZE, CELLS, NODES)
    atom_proj = projector.reshape(PARTS_SIZE, SLOTS, NPROJ, SUPPORT)
    atom_coupling = coupling.reshape(PARTS_SIZE, SLOTS, NPROJ)
    starts = atom_start.reshape(PARTS_SIZE, SLOTS)

    def scan_step(pending, inputs_now):
        own_block, head_rows, tail_rows, mats, nodes_now, proj_now, coup_now, start_now, count_now = inputs_now
        extended = jnp.concatenate([head_rows, own_block, tail_rows], axis=0)
        contributions = partition_apply(extended, mats, nodes_now, proj_now, coup_now, start_now, count_now)
        owned_rows = contributions[GHOST:GHOST + OWN]
        owned_rows = jnp.concatenate([owned_rows[:GHOST] + pending, owned_rows[GHOST:]], axis=0)
        return contributions[GHOST + OWN:], (owned_rows, contributions[:GHOST])

    start_value = jnp.zeros((GHOST, NBANDS), jnp.float32)
    last_pending, (owned_all, left_parts) = lax.scan(scan_step, start_value, (blocks, before, after, matrices, node_map, atom_proj, atom_coupling, starts, atom_count))
    incoming = jnp.concatenate([left_parts[1:], zero_block], axis=0)
    owned_all = jnp.concatenate([owned_all[:, :OWN - GHOST], owned_all[:, OWN - GHOST:] + incoming], axis=1)
    return owned_all.reshape(TOTAL, NBANDS)


def reference(wavefunctions, cell_matrix, connectivity, projector, coupling, atom_start, atom_count):
    first_image = hamiltonian(wavefunctions, cell_matrix, connectivity, projector, coupling, atom_start, atom_count)
    step_one = (first_image - filter_center * wavefunctions) / filter_half
    second_image = hamiltonian(step_one, cell_matrix, connectivity, projector, coupling, atom_start, atom_count)
    filtered = 2.0 * (second_image - filter_center * step_one) / filter_half - wavefunctions
    return filtered
```

```python
import jax
import jax.numpy as jnp
from jax import lax
from jax.sharding import PartitionSpec as P

GHOST = 128


filter_center = 0.25
filter_half = 2.0
highest = lax.Precision.HIGHEST


def from_left(x, axis):
    count = lax.axis_size(axis)
    return lax.ppermute(x, axis, [(i, i + 1) for i in range(count - 1)])


def from_right(x, axis):
    count = lax.axis_size(axis)
    return lax.ppermute(x, axis, [(i + 1, i) for i in range(count - 1)])


def gather_band(piece):
    count = lax.axis_size("band")
    me = lax.axis_index("band")
    pieces = [piece]
    for k in range(1, count):
        pieces.append(
            lax.ppermute(piece, "band", [(i, (i + k) % count) for i in range(count)])
        )
    stacked = jnp.stack(pieces)
    order = (me - jnp.arange(count)) % count
    ordered = jnp.take(stacked, order, axis=0)
    slots, channels, width = piece.shape
    return ordered.transpose(1, 2, 0, 3).reshape(slots, channels, count * width)


def local_operator(cell_matrix, connectivity, projector_full, coupling, atom_start, atom_count, ext):
    rows = jnp.arange(ext, dtype=connectivity.dtype)
    onehot = (connectivity[:, :, None] == rows[None, None, :]).astype(jnp.float32)
    moved = jnp.einsum("cij,cjq->ciq", cell_matrix, onehot, precision=highest)
    cells = jnp.einsum("cip,ciq->pq", onehot, moved, precision=highest)
    slots, channels, support = projector_full.shape
    live = (jnp.arange(slots) < atom_count[0]).astype(jnp.float32)
    weights = (coupling * live[:, None]).reshape(slots * channels)
    placed = []
    for slot_index in range(slots):
        placed.append(
            lax.dynamic_update_slice(
                jnp.zeros((channels, ext), jnp.float32),
                projector_full[slot_index],
                (0, atom_start[slot_index]),
            )
        )
    placed = jnp.concatenate(placed, axis=0)
    atoms = jnp.dot((placed * weights[:, None]).T, placed, precision=highest)
    return cells + atoms


def on_device(
    wavefunctions, cell_matrix, connectivity, projector, coupling, atom_start, atom_count
):
    own = wavefunctions.shape[0]
    g = GHOST
    ext = own + 2 * g
    count = lax.axis_size("dom")
    me = lax.axis_index("dom")

    low = from_left(wavefunctions[own - g :], "dom")
    high = from_right(wavefunctions[:g], "dom")
    extended = jnp.concatenate([low, wavefunctions, high], axis=0)

    projector_full = gather_band(projector)
    operator = local_operator(
        cell_matrix, connectivity, projector_full, coupling, atom_start, atom_count, ext
    )

    first = jnp.dot(operator, extended, precision=highest)
    left_sums = from_left(first[ext - 2 * g :], "dom")
    right_sums = from_right(first[: 2 * g], "dom")
    zeros_side = jnp.zeros((ext - 2 * g, first.shape[1]), jnp.float32)
    first_image = (
        first
        + jnp.concatenate([left_sums, zeros_side], axis=0)
        + jnp.concatenate([zeros_side, right_sums], axis=0)
    )
    step_ext = (first_image - filter_center * extended) / filter_half
    row = lax.broadcasted_iota(jnp.int32, (ext, 1), 0)
    keep = jnp.logical_and(
        jnp.logical_or(row >= g, me > 0), jnp.logical_or(row < ext - g, me < count - 1)
    )
    step_ext = jnp.where(keep, step_ext, 0.0)
    step_one = step_ext[g : g + own]

    second = jnp.dot(operator, step_ext, precision=highest)
    from_before = from_left(second[ext - g :], "dom")
    from_after = from_right(second[:g], "dom")
    owned = second[g : g + own]
    zeros_own = jnp.zeros((own - g, owned.shape[1]), jnp.float32)
    second_image = (
        owned
        + jnp.concatenate([from_before, zeros_own], axis=0)
        + jnp.concatenate([zeros_own, from_after], axis=0)
    )
    filtered = 2.0 * (second_image - filter_center * step_one) / filter_half - wavefunctions
    return filtered


def solution(mesh):
    return jax.shard_map(
        on_device,
        mesh=mesh,
        in_specs=(
            P("dom", "band"),
            P("dom", None, None),
            P("dom", None),
            P("dom", None, "band"),
            P("dom", None),
            P("dom"),
            P("dom"),
        ),
        out_specs=P("dom", "band"),
        check_vma=False,
    )
```

```python
import jax
import jax.numpy as jnp
from jax import lax
from jax.sharding import PartitionSpec as P

GHOST = 128


filter_center = 0.25
filter_half = 2.0
highest = lax.Precision.HIGHEST


def from_left(x, axis):
    count = lax.axis_size(axis)
    return lax.ppermute(x, axis, [(i, i + 1) for i in range(count - 1)])


def from_right(x, axis):
    count = lax.axis_size(axis)
    return lax.ppermute(x, axis, [(i + 1, i) for i in range(count - 1)])


def gather_band(piece):
    count = lax.axis_size("band")
    copies = jnp.broadcast_to(piece[None], (count,) + piece.shape)
    return lax.all_to_all(copies, "band", 0, 0, tiled=True)


def split_bf16(x):
    hi = lax.reduce_precision(x, exponent_bits=8, mantissa_bits=7)
    rest = x - hi
    mid = lax.reduce_precision(rest, exponent_bits=8, mantissa_bits=7)
    lo = rest - mid
    return [part.astype(jnp.bfloat16) for part in (hi, mid, lo)]


def cell_operator(cell_matrix, connectivity, ext):
    cells = cell_matrix.shape[0]
    rows = jnp.arange(ext, dtype=connectivity.dtype)
    onehot = (connectivity[:, :, None] == rows[None, None, :]).astype(jnp.bfloat16)
    parts = jnp.concatenate(split_bf16(cell_matrix), axis=2)
    moved = jnp.einsum("cip,cij->cpj", onehot, parts, preferred_element_type=jnp.float32)
    moved = moved.astype(jnp.bfloat16)
    nodes = connectivity.shape[1]
    left = moved.reshape(cells, ext, 3, nodes).transpose(1, 0, 2, 3).reshape(ext, cells * 3 * nodes)
    right = jnp.broadcast_to(onehot[:, None], (cells, 3, nodes, ext)).reshape(cells * 3 * nodes, ext)
    return jnp.dot(left, right, preferred_element_type=jnp.float32)


def atom_rows(pieces, coupling, atom_start, atom_count, ext):
    count, slots, channels, width = pieces.shape
    t = lax.broadcasted_iota(jnp.int32, (count, slots, width, ext), 2)
    q = lax.broadcasted_iota(jnp.int32, (count, slots, width, ext), 3)
    k = lax.broadcasted_iota(jnp.int32, (count, slots, width, ext), 0)
    first = atom_start.astype(jnp.int32)[None, :, None, None]
    shift = (q == first + k * width + t).astype(jnp.float32)
    placed = jnp.einsum("kscj,ksjq->scq", pieces, shift, precision=highest)
    live = (jnp.arange(slots, dtype=jnp.int32)[:, None] < atom_count.astype(jnp.int32)[None, :])
    weights = coupling * live.astype(jnp.float32)
    return placed.reshape(slots * channels, ext), weights.reshape(slots * channels)


def on_device(
    wavefunctions, cell_matrix, connectivity, projector, coupling, atom_start, atom_count
):
    own = wavefunctions.shape[0]
    g = GHOST
    ext = own + 2 * g
    count = lax.axis_size("dom")
    me = lax.axis_index("dom")

    low = from_left(wavefunctions[own - g :], "dom")
    high = from_right(wavefunctions[:g], "dom")
    extended = jnp.concatenate([low, wavefunctions, high], axis=0)

    cells = cell_operator(cell_matrix, connectivity, ext)
    placed, weights = atom_rows(gather_band(projector), coupling, atom_start, atom_count, ext)
    operator = cells + jnp.dot((placed * weights[:, None]).T, placed, precision=highest)

    coefficients = jnp.dot(placed, extended, precision=highest) * weights[:, None]
    first = jnp.dot(cells, extended, precision=highest) + jnp.dot(
        placed.T, coefficients, precision=highest
    )
    left_sums = from_left(first[ext - 2 * g :], "dom")
    right_sums = from_right(first[: 2 * g], "dom")
    zeros_side = jnp.zeros((ext - 2 * g, first.shape[1]), jnp.float32)
    first_image = (
        first
        + jnp.concatenate([left_sums, zeros_side], axis=0)
        + jnp.concatenate([zeros_side, right_sums], axis=0)
    )
    step_ext = (first_image - filter_center * extended) / filter_half
    row = lax.broadcasted_iota(jnp.int32, (ext, 1), 0)
    keep = jnp.logical_and(
        jnp.logical_or(row >= g, me > 0), jnp.logical_or(row < ext - g, me < count - 1)
    )
    step_ext = jnp.where(keep, step_ext, 0.0)
    step_one = step_ext[g : g + own]

    second = jnp.dot(operator, step_ext, precision=highest)
    from_before = from_left(second[ext - g :], "dom")
    from_after = from_right(second[:g], "dom")
    owned = second[g : g + own]
    zeros_own = jnp.zeros((own - g, owned.shape[1]), jnp.float32)
    second_image = (
        owned
        + jnp.concatenate([from_before, zeros_own], axis=0)
        + jnp.concatenate([zeros_own, from_after], axis=0)
    )
    filtered = 2.0 * (second_image - filter_center * step_one) / filter_half - wavefunctions
    return filtered


def solution(mesh):
    return jax.shard_map(
        on_device,
        mesh=mesh,
        in_specs=(
            P("dom", "band"),
            P("dom", None, None),
            P("dom", None),
            P("dom", None, "band"),
            P("dom", None),
            P("dom"),
            P("dom"),
        ),
        out_specs=P("dom", "band"),
        check_vma=False,
    )
```

```python
import jax
import jax.numpy as jnp
from jax import lax
from jax.sharding import PartitionSpec as P

GHOST = 128


filter_center = 0.25
filter_half = 2.0
highest = lax.Precision.HIGHEST


def from_left(x, axis):
    count = lax.axis_size(axis)
    return lax.ppermute(x, axis, [(i, i + 1) for i in range(count - 1)])


def from_right(x, axis):
    count = lax.axis_size(axis)
    return lax.ppermute(x, axis, [(i + 1, i) for i in range(count - 1)])


def gather_band(piece):
    count = lax.axis_size("band")
    copies = jnp.broadcast_to(piece[None], (count,) + piece.shape)
    return lax.all_to_all(copies, "band", 0, 0, tiled=True)


def split_parts(x):
    hi = lax.reduce_precision(x, exponent_bits=8, mantissa_bits=7)
    rest = x - hi
    mid = lax.reduce_precision(rest, exponent_bits=8, mantissa_bits=7)
    lo = rest - mid
    return jnp.concatenate([hi, mid, lo], axis=0).astype(jnp.bfloat16)


def select_rows(tripled, x):
    return jnp.dot(tripled, split_parts(x), preferred_element_type=jnp.float32)


def atom_rows(pieces, coupling, atom_start, atom_count, ext):
    count, slots, channels, width = pieces.shape
    t = lax.broadcasted_iota(jnp.int32, (count, slots, width, ext), 2)
    q = lax.broadcasted_iota(jnp.int32, (count, slots, width, ext), 3)
    k = lax.broadcasted_iota(jnp.int32, (count, slots, width, ext), 0)
    first = atom_start.astype(jnp.int32)[None, :, None, None]
    shift = (q == first + k * width + t).astype(jnp.float32)
    placed = jnp.einsum("kscj,ksjq->scq", pieces, shift, precision=highest)
    live = jnp.arange(slots, dtype=jnp.int32)[:, None] < atom_count.astype(jnp.int32)[None, :]
    weights = coupling * live.astype(jnp.float32)
    return placed.reshape(slots * channels, ext), weights.reshape(slots * channels)


def make_operator(cell_matrix, connectivity, placed, weights, ext):
    cells, nodes, _ = cell_matrix.shape
    rows = jnp.arange(ext, dtype=connectivity.dtype)
    onehot = (connectivity.reshape(cells * nodes)[:, None] == rows[None, :]).astype(jnp.bfloat16)
    gather3 = jnp.concatenate([onehot] * 3, axis=1)
    scatter3 = jnp.concatenate([onehot.T] * 3, axis=1)

    def apply(x):
        gathered = select_rows(gather3, x).reshape(cells, nodes, x.shape[1])
        local = jnp.einsum(
            "cij,cjb->cib", cell_matrix, gathered, precision=highest,
            preferred_element_type=jnp.float32,
        )
        out = select_rows(scatter3, local.reshape(cells * nodes, x.shape[1]))
        coefficients = jnp.dot(placed, x, precision=highest) * weights[:, None]
        return out + jnp.dot(placed.T, coefficients, precision=highest)

    return apply


def on_device(
    wavefunctions, cell_matrix, connectivity, projector, coupling, atom_start, atom_count
):
    own = wavefunctions.shape[0]
    g = GHOST
    ext = own + 2 * g
    count = lax.axis_size("dom")
    me = lax.axis_index("dom")

    low = from_left(wavefunctions[own - g :], "dom")
    high = from_right(wavefunctions[:g], "dom")
    extended = jnp.concatenate([low, wavefunctions, high], axis=0)

    placed, weights = atom_rows(gather_band(projector), coupling, atom_start, atom_count, ext)
    apply = make_operator(cell_matrix, connectivity, placed, weights, ext)

    first = apply(extended)
    left_sums = from_left(first[ext - 2 * g :], "dom")
    right_sums = from_right(first[: 2 * g], "dom")
    zeros_side = jnp.zeros((ext - 2 * g, first.shape[1]), jnp.float32)
    first_image = (
        first
        + jnp.concatenate([left_sums, zeros_side], axis=0)
        + jnp.concatenate([zeros_side, right_sums], axis=0)
    )
    step_ext = (first_image - filter_center * extended) / filter_half
    row = lax.broadcasted_iota(jnp.int32, (ext, 1), 0)
    keep = jnp.logical_and(
        jnp.logical_or(row >= g, me > 0), jnp.logical_or(row < ext - g, me < count - 1)
    )
    step_ext = jnp.where(keep, step_ext, 0.0)
    step_one = step_ext[g : g + own]

    second = apply(step_ext)
    from_before = from_left(second[ext - g :], "dom")
    from_after = from_right(second[:g], "dom")
    owned = second[g : g + own]
    zeros_own = jnp.zeros((own - g, owned.shape[1]), jnp.float32)
    second_image = (
        owned
        + jnp.concatenate([from_before, zeros_own], axis=0)
        + jnp.concatenate([zeros_own, from_after], axis=0)
    )
    filtered = 2.0 * (second_image - filter_center * step_one) / filter_half - wavefunctions
    return filtered


def solution(mesh):
    return jax.shard_map(
        on_device,
        mesh=mesh,
        in_specs=(
            P("dom", "band"),
            P("dom", None, None),
            P("dom", None),
            P("dom", None, "band"),
            P("dom", None),
            P("dom"),
            P("dom"),
        ),
        out_specs=P("dom", "band"),
        check_vma=False,
    )
```

```python
import jax
import jax.numpy as jnp
from jax import lax
from jax.sharding import PartitionSpec as P

GHOST = 128


filter_center = 0.25
filter_half = 2.0
highest = lax.Precision.HIGHEST


def from_left(x, axis):
    count = lax.axis_size(axis)
    return lax.ppermute(x, axis, [(i, i + 1) for i in range(count - 1)])


def from_right(x, axis):
    count = lax.axis_size(axis)
    return lax.ppermute(x, axis, [(i + 1, i) for i in range(count - 1)])


def gather_band(piece):
    count = lax.axis_size("band")
    copies = jnp.broadcast_to(piece[None], (count,) + piece.shape)
    return lax.all_to_all(copies, "band", 0, 0, tiled=True)


def atom_rows(pieces, coupling, atom_start, atom_count, ext):
    count, slots, channels, width = pieces.shape
    t = lax.broadcasted_iota(jnp.int32, (count, slots, width, ext), 2)
    q = lax.broadcasted_iota(jnp.int32, (count, slots, width, ext), 3)
    k = lax.broadcasted_iota(jnp.int32, (count, slots, width, ext), 0)
    first = atom_start.astype(jnp.int32)[None, :, None, None]
    shift = (q == first + k * width + t).astype(jnp.float32)
    placed = jnp.einsum("kscj,ksjq->scq", pieces, shift, precision=highest)
    live = jnp.arange(slots, dtype=jnp.int32)[:, None] < atom_count.astype(jnp.int32)[None, :]
    weights = coupling * live.astype(jnp.float32)
    return placed.reshape(slots * channels, ext), weights.reshape(slots * channels)


def cell_operator(cell_matrix, connectivity, ext):
    cells, nodes, _ = cell_matrix.shape
    rows = jnp.arange(ext, dtype=connectivity.dtype)
    onehot = (connectivity[:, :, None] == rows[None, None, :]).astype(jnp.float32)
    total = None
    for c in range(cells):
        moved = jnp.dot(cell_matrix[c], onehot[c], precision=lax.Precision.HIGH)
        part = lax.dot_general(
            onehot[c], moved, (((0,), (0,)), ((), ())), precision=lax.Precision.HIGH
        )
        total = part if total is None else total + part
    return total


def on_device(
    wavefunctions, cell_matrix, connectivity, projector, coupling, atom_start, atom_count
):
    own = wavefunctions.shape[0]
    g = GHOST
    ext = own + 2 * g
    count = lax.axis_size("dom")
    me = lax.axis_index("dom")

    low = from_left(wavefunctions[own - g :], "dom")
    high = from_right(wavefunctions[:g], "dom")
    extended = jnp.concatenate([low, wavefunctions, high], axis=0)

    placed, weights = atom_rows(gather_band(projector), coupling, atom_start, atom_count, ext)
    cells = cell_operator(cell_matrix, connectivity, ext)
    operator = cells + jnp.dot((placed * weights[:, None]).T, placed, precision=highest)

    coefficients = jnp.dot(placed, extended, precision=highest) * weights[:, None]
    first = jnp.dot(cells, extended, precision=highest) + jnp.dot(
        placed.T, coefficients, precision=highest
    )
    left_sums = from_left(first[ext - 2 * g :], "dom")
    right_sums = from_right(first[: 2 * g], "dom")
    zeros_side = jnp.zeros((ext - 2 * g, first.shape[1]), jnp.float32)
    first_image = (
        first
        + jnp.concatenate([left_sums, zeros_side], axis=0)
        + jnp.concatenate([zeros_side, right_sums], axis=0)
    )
    step_ext = (first_image - filter_center * extended) / filter_half
    row = lax.broadcasted_iota(jnp.int32, (ext, 1), 0)
    keep = jnp.logical_and(
        jnp.logical_or(row >= g, me > 0), jnp.logical_or(row < ext - g, me < count - 1)
    )
    step_ext = jnp.where(keep, step_ext, 0.0)
    step_one = step_ext[g : g + own]

    second = jnp.dot(operator, step_ext, precision=highest)
    from_before = from_left(second[ext - g :], "dom")
    from_after = from_right(second[:g], "dom")
    owned = second[g : g + own]
    zeros_own = jnp.zeros((own - g, owned.shape[1]), jnp.float32)
    second_image = (
        owned
        + jnp.concatenate([from_before, zeros_own], axis=0)
        + jnp.concatenate([zeros_own, from_after], axis=0)
    )
    filtered = 2.0 * (second_image - filter_center * step_one) / filter_half - wavefunctions
    return filtered


def solution(mesh):
    return jax.shard_map(
        on_device,
        mesh=mesh,
        in_specs=(
            P("dom", "band"),
            P("dom", None, None),
            P("dom", None),
            P("dom", None, "band"),
            P("dom", None),
            P("dom"),
            P("dom"),
        ),
        out_specs=P("dom", "band"),
        check_vma=False,
    )
```

```python
import jax
import jax.numpy as jnp
from jax import lax
from jax.sharding import PartitionSpec as P

GHOST = 128


filter_center = 0.25
filter_half = 2.0
highest = lax.Precision.HIGHEST


def from_left(x, axis):
    count = lax.axis_size(axis)
    return lax.ppermute(x, axis, [(i, i + 1) for i in range(count - 1)])


def from_right(x, axis):
    count = lax.axis_size(axis)
    return lax.ppermute(x, axis, [(i + 1, i) for i in range(count - 1)])


def gather_band(piece):
    count = lax.axis_size("band")
    me = lax.axis_index("band")
    pieces = [piece]
    for k in range(1, count):
        pieces.append(
            lax.ppermute(piece, "band", [(i, (i + k) % count) for i in range(count)])
        )
    stacked = jnp.stack(pieces)
    order = (me - jnp.arange(count)) % count
    ordered = jnp.take(stacked, order, axis=0)
    slots, channels, width = piece.shape
    return ordered.transpose(1, 2, 0, 3).reshape(slots, channels, count * width)


def shift_right(x, amount, bits):
    for b in range(bits):
        step = 1 << b
        moved = jnp.concatenate(
            [jnp.zeros(x.shape[:-1] + (step,), x.dtype), x[..., :-step]], axis=-1
        )
        x = jnp.where(((amount >> b) & 1)[:, None, None] == 1, moved, x)
    return x


def atom_rows(projector_full, coupling, atom_start, atom_count, ext):
    slots, channels, support = projector_full.shape
    first = jnp.clip(atom_start.astype(jnp.int32), 0, ext - support)
    padded = jnp.concatenate(
        [projector_full, jnp.zeros((slots, channels, ext - support), projector_full.dtype)], axis=-1
    )
    placed = shift_right(padded, first, (ext - support).bit_length())
    live = jnp.arange(slots, dtype=jnp.int32)[:, None] < atom_count.astype(jnp.int32)[None, :]
    weights = coupling * live.astype(jnp.float32)
    return placed.reshape(slots * channels, ext), weights.reshape(slots * channels)


def split_parts(x, axis):
    hi = lax.reduce_precision(x, exponent_bits=8, mantissa_bits=7)
    rest = x - hi
    mid = lax.reduce_precision(rest, exponent_bits=8, mantissa_bits=7)
    lo = rest - mid
    return jnp.concatenate([hi, mid, lo], axis=axis).astype(jnp.bfloat16)


def cell_operator(cell_matrix, connectivity, ext):
    cells, nodes, _ = cell_matrix.shape
    rows = jnp.arange(ext, dtype=connectivity.dtype)
    onehot = (connectivity[:, :, None] == rows[None, None, :]).astype(jnp.bfloat16)
    onehot_t = (rows[None, :, None] == connectivity[:, None, :]).astype(jnp.bfloat16)
    lefts, rights = [], []
    for c in range(cells):
        moved = jnp.dot(
            split_parts(cell_matrix[c], 1),
            jnp.concatenate([onehot[c]] * 3, axis=0),
            preferred_element_type=jnp.float32,
        )
        lefts += [onehot_t[c]] * 3
        rights.append(split_parts(moved, 0))
    return jnp.dot(
        jnp.concatenate(lefts, axis=1),
        jnp.concatenate(rights, axis=0),
        preferred_element_type=jnp.float32,
    )


def on_device(
    wavefunctions, cell_matrix, connectivity, projector, coupling, atom_start, atom_count
):
    own = wavefunctions.shape[0]
    g = GHOST
    ext = own + 2 * g
    count = lax.axis_size("dom")
    me = lax.axis_index("dom")

    low = from_left(wavefunctions[own - g :], "dom")
    high = from_right(wavefunctions[:g], "dom")
    extended = jnp.concatenate([low, wavefunctions, high], axis=0)

    placed, weights = atom_rows(gather_band(projector), coupling, atom_start, atom_count, ext)
    cells = cell_operator(cell_matrix, connectivity, ext)
    operator = cells + jnp.dot((placed * weights[:, None]).T, placed, precision=highest)

    coefficients = jnp.dot(placed, extended, precision=highest) * weights[:, None]
    first = jnp.dot(cells, extended, precision=lax.Precision.HIGH) + jnp.dot(
        placed.T, coefficients, precision=highest
    )
    left_sums = from_left(first[ext - 2 * g :], "dom")
    right_sums = from_right(first[: 2 * g], "dom")
    zeros_side = jnp.zeros((ext - 2 * g, first.shape[1]), jnp.float32)
    first_image = (
        first
        + jnp.concatenate([left_sums, zeros_side], axis=0)
        + jnp.concatenate([zeros_side, right_sums], axis=0)
    )
    step_ext = (first_image - filter_center * extended) / filter_half
    row = lax.broadcasted_iota(jnp.int32, (ext, 1), 0)
    keep = jnp.logical_and(
        jnp.logical_or(row >= g, me > 0), jnp.logical_or(row < ext - g, me < count - 1)
    )
    step_ext = jnp.where(keep, step_ext, 0.0)
    step_one = step_ext[g : g + own]

    second = jnp.dot(operator, step_ext, precision=lax.Precision.HIGH)
    from_before = from_left(second[ext - g :], "dom")
    from_after = from_right(second[:g], "dom")
    owned = second[g : g + own]
    zeros_own = jnp.zeros((own - g, owned.shape[1]), jnp.float32)
    second_image = (
        owned
        + jnp.concatenate([from_before, zeros_own], axis=0)
        + jnp.concatenate([zeros_own, from_after], axis=0)
    )
    filtered = 2.0 * (second_image - filter_center * step_one) / filter_half - wavefunctions
    return filtered


def solution(mesh):
    return jax.shard_map(
        on_device,
        mesh=mesh,
        in_specs=(
            P("dom", "band"),
            P("dom", None, None),
            P("dom", None),
            P("dom", None, "band"),
            P("dom", None),
            P("dom"),
            P("dom"),
        ),
        out_specs=P("dom", "band"),
        check_vma=False,
    )
```

```python
import jax
import jax.numpy as jnp
from jax import lax
from jax.sharding import PartitionSpec as P

GHOST = 128


filter_center = 0.25
filter_half = 2.0
highest = lax.Precision.HIGHEST


def from_left(x, axis):
    count = lax.axis_size(axis)
    return lax.ppermute(x, axis, [(i, i + 1) for i in range(count - 1)])


def from_right(x, axis):
    count = lax.axis_size(axis)
    return lax.ppermute(x, axis, [(i + 1, i) for i in range(count - 1)])


def gather_band(piece):
    count = lax.axis_size("band")
    me = lax.axis_index("band")
    pieces = [piece]
    for k in range(1, count):
        pieces.append(
            lax.ppermute(piece, "band", [(i, (i + k) % count) for i in range(count)])
        )
    stacked = jnp.stack(pieces)
    order = (me - jnp.arange(count)) % count
    ordered = jnp.take(stacked, order, axis=0)
    slots, channels, width = piece.shape
    return ordered.transpose(1, 2, 0, 3).reshape(slots, channels, count * width)


def shift_right(x, amount, bits):
    for b in range(bits):
        step = 1 << b
        moved = jnp.concatenate(
            [jnp.zeros(x.shape[:-1] + (step,), x.dtype), x[..., :-step]], axis=-1
        )
        x = jnp.where(((amount >> b) & 1)[:, None, None] == 1, moved, x)
    return x


def atom_rows(projector_full, coupling, atom_start, atom_count, ext):
    slots, channels, support = projector_full.shape
    first = jnp.clip(atom_start.astype(jnp.int32), 0, ext - support)
    padded = jnp.concatenate(
        [projector_full, jnp.zeros((slots, channels, ext - support), projector_full.dtype)], axis=-1
    )
    placed = shift_right(padded, first, (ext - support).bit_length())
    live = jnp.arange(slots, dtype=jnp.int32)[:, None] < atom_count.astype(jnp.int32)[None, :]
    weights = coupling * live.astype(jnp.float32)
    return placed.reshape(slots * channels, ext), weights.reshape(slots * channels)


def split_parts(x, axis):
    hi = lax.reduce_precision(x, exponent_bits=8, mantissa_bits=7)
    rest = x - hi
    mid = lax.reduce_precision(rest, exponent_bits=8, mantissa_bits=7)
    lo = rest - mid
    return jnp.concatenate([hi, mid, lo], axis=axis).astype(jnp.bfloat16)


def cell_operator(cell_matrix, connectivity, ext):
    cells, nodes, _ = cell_matrix.shape
    rows = jnp.arange(ext, dtype=connectivity.dtype)
    onehot = (connectivity[:, :, None] == rows[None, None, :]).astype(jnp.bfloat16)
    total = None
    for c in range(cells):
        moved = jnp.dot(
            split_parts(cell_matrix[c], 1),
            jnp.concatenate([onehot[c]] * 3, axis=0),
            preferred_element_type=jnp.float32,
        )
        part = lax.dot_general(
            onehot[c].astype(jnp.float32), moved, (((0,), (0,)), ((), ())),
            precision=lax.Precision.HIGH,
        )
        total = part if total is None else total + part
    return total


def on_device(
    wavefunctions, cell_matrix, connectivity, projector, coupling, atom_start, atom_count
):
    own = wavefunctions.shape[0]
    g = GHOST
    ext = own + 2 * g
    count = lax.axis_size("dom")
    me = lax.axis_index("dom")

    low = from_left(wavefunctions[own - g :], "dom")
    high = from_right(wavefunctions[:g], "dom")
    extended = jnp.concatenate([low, wavefunctions, high], axis=0)

    placed, weights = atom_rows(gather_band(projector), coupling, atom_start, atom_count, ext)
    cells = cell_operator(cell_matrix, connectivity, ext)
    operator = cells + jnp.dot((placed * weights[:, None]).T, placed, precision=highest)

    coefficients = jnp.dot(placed, extended, precision=highest) * weights[:, None]
    first = jnp.dot(cells, extended, precision=lax.Precision.HIGH) + jnp.dot(
        placed.T, coefficients, precision=highest
    )
    left_sums = from_left(first[ext - 2 * g :], "dom")
    right_sums = from_right(first[: 2 * g], "dom")
    zeros_side = jnp.zeros((ext - 2 * g, first.shape[1]), jnp.float32)
    first_image = (
        first
        + jnp.concatenate([left_sums, zeros_side], axis=0)
        + jnp.concatenate([zeros_side, right_sums], axis=0)
    )
    step_ext = (first_image - filter_center * extended) / filter_half
    row = lax.broadcasted_iota(jnp.int32, (ext, 1), 0)
    keep = jnp.logical_and(
        jnp.logical_or(row >= g, me > 0), jnp.logical_or(row < ext - g, me < count - 1)
    )
    step_ext = jnp.where(keep, step_ext, 0.0)
    step_one = step_ext[g : g + own]

    second = jnp.dot(operator, step_ext, precision=lax.Precision.HIGH)
    from_before = from_left(second[ext - g :], "dom")
    from_after = from_right(second[:g], "dom")
    owned = second[g : g + own]
    zeros_own = jnp.zeros((own - g, owned.shape[1]), jnp.float32)
    second_image = (
        owned
        + jnp.concatenate([from_before, zeros_own], axis=0)
        + jnp.concatenate([zeros_own, from_after], axis=0)
    )
    filtered = 2.0 * (second_image - filter_center * step_one) / filter_half - wavefunctions
    return filtered


def solution(mesh):
    return jax.shard_map(
        on_device,
        mesh=mesh,
        in_specs=(
            P("dom", "band"),
            P("dom", None, None),
            P("dom", None),
            P("dom", None, "band"),
            P("dom", None),
            P("dom"),
            P("dom"),
        ),
        out_specs=P("dom", "band"),
        check_vma=False,
    )
```

```python
import jax
import jax.numpy as jnp
from jax import lax
from jax.sharding import PartitionSpec as P

GHOST = 128


filter_center = 0.25
filter_half = 2.0
highest = lax.Precision.HIGHEST


def from_left(x, axis):
    count = lax.axis_size(axis)
    return lax.ppermute(x, axis, [(i, i + 1) for i in range(count - 1)])


def from_right(x, axis):
    count = lax.axis_size(axis)
    return lax.ppermute(x, axis, [(i + 1, i) for i in range(count - 1)])


def gather_band(piece):
    count = lax.axis_size("band")
    me = lax.axis_index("band")
    pieces = [piece]
    for k in range(1, count):
        pieces.append(
            lax.ppermute(piece, "band", [(i, (i + k) % count) for i in range(count)])
        )
    stacked = jnp.stack(pieces)
    order = (me - jnp.arange(count)) % count
    ordered = jnp.take(stacked, order, axis=0)
    slots, channels, width = piece.shape
    return ordered.transpose(1, 2, 0, 3).reshape(slots, channels, count * width)


def shift_right(x, amount, bits):
    for b in range(bits):
        step = 1 << b
        moved = jnp.concatenate(
            [jnp.zeros(x.shape[:-1] + (step,), x.dtype), x[..., :-step]], axis=-1
        )
        x = jnp.where(((amount >> b) & 1)[:, None, None] == 1, moved, x)
    return x


def atom_rows(projector_full, coupling, atom_start, atom_count, ext):
    slots, channels, support = projector_full.shape
    first = jnp.clip(atom_start.astype(jnp.int32), 0, ext - support)
    padded = jnp.concatenate(
        [projector_full, jnp.zeros((slots, channels, ext - support), projector_full.dtype)], axis=-1
    )
    placed = shift_right(padded, first, (ext - support).bit_length())
    live = jnp.arange(slots, dtype=jnp.int32)[:, None] < atom_count.astype(jnp.int32)[None, :]
    weights = coupling * live.astype(jnp.float32)
    return placed.reshape(slots * channels, ext), weights.reshape(slots * channels)


def cell_operator(cell_matrix, connectivity, ext):
    cells, nodes, _ = cell_matrix.shape
    rows = jnp.arange(ext, dtype=connectivity.dtype)
    onehot = (connectivity[:, :, None] == rows[None, None, :]).astype(jnp.float32)
    total = None
    for c in range(cells):
        moved = jnp.dot(cell_matrix[c], onehot[c], precision=lax.Precision.HIGH)
        part = lax.dot_general(
            onehot[c], moved, (((0,), (0,)), ((), ())), precision=lax.Precision.HIGH
        )
        total = part if total is None else total + part
    return total


def on_device(
    wavefunctions, cell_matrix, connectivity, projector, coupling, atom_start, atom_count
):
    own = wavefunctions.shape[0]
    g = GHOST
    ext = own + 2 * g
    count = lax.axis_size("dom")
    me = lax.axis_index("dom")

    low = from_left(wavefunctions[own - g :], "dom")
    high = from_right(wavefunctions[:g], "dom")
    extended = jnp.concatenate([low, wavefunctions, high], axis=0)

    placed, weights = atom_rows(gather_band(projector), coupling, atom_start, atom_count, ext)
    cells = cell_operator(cell_matrix, connectivity, ext)
    operator = cells + jnp.dot((placed * weights[:, None]).T, placed, precision=highest)

    coefficients = jnp.dot(placed, extended, precision=highest) * weights[:, None]
    first = jnp.dot(cells, extended, precision=lax.Precision.HIGH) + jnp.dot(
        placed.T, coefficients, precision=highest
    )
    left_sums = from_left(first[ext - 2 * g :], "dom")
    right_sums = from_right(first[: 2 * g], "dom")
    zeros_side = jnp.zeros((ext - 2 * g, first.shape[1]), jnp.float32)
    first_image = (
        first
        + jnp.concatenate([left_sums, zeros_side], axis=0)
        + jnp.concatenate([zeros_side, right_sums], axis=0)
    )
    step_ext = (first_image - filter_center * extended) / filter_half
    row = lax.broadcasted_iota(jnp.int32, (ext, 1), 0)
    keep = jnp.logical_and(
        jnp.logical_or(row >= g, me > 0), jnp.logical_or(row < ext - g, me < count - 1)
    )
    step_ext = jnp.where(keep, step_ext, 0.0)
    step_one = step_ext[g : g + own]

    second = jnp.dot(operator, step_ext, precision=lax.Precision.HIGH)
    from_before = from_left(second[ext - g :], "dom")
    from_after = from_right(second[:g], "dom")
    owned = second[g : g + own]
    zeros_own = jnp.zeros((own - g, owned.shape[1]), jnp.float32)
    second_image = (
        owned
        + jnp.concatenate([from_before, zeros_own], axis=0)
        + jnp.concatenate([zeros_own, from_after], axis=0)
    )
    filtered = 2.0 * (second_image - filter_center * step_one) / filter_half - wavefunctions
    return filtered


def solution(mesh):
    return jax.shard_map(
        on_device,
        mesh=mesh,
        in_specs=(
            P("dom", "band"),
            P("dom", None, None),
            P("dom", None),
            P("dom", None, "band"),
            P("dom", None),
            P("dom"),
            P("dom"),
        ),
        out_specs=P("dom", "band"),
        check_vma=False,
    )
```

```python
import jax
import jax.numpy as jnp
from jax import lax
from jax.sharding import PartitionSpec as P

GHOST = 128


filter_center = 0.25
filter_half = 2.0
highest = lax.Precision.HIGHEST


def from_left(x, axis):
    count = lax.axis_size(axis)
    return lax.ppermute(x, axis, [(i, i + 1) for i in range(count - 1)])


def from_right(x, axis):
    count = lax.axis_size(axis)
    return lax.ppermute(x, axis, [(i + 1, i) for i in range(count - 1)])


def gather_band(piece):
    count = lax.axis_size("band")
    me = lax.axis_index("band")
    pieces = [piece]
    for k in range(1, count):
        pieces.append(
            lax.ppermute(piece, "band", [(i, (i + k) % count) for i in range(count)])
        )
    stacked = jnp.stack(pieces)
    order = (me - jnp.arange(count)) % count
    ordered = jnp.take(stacked, order, axis=0)
    slots, channels, width = piece.shape
    return ordered.transpose(1, 2, 0, 3).reshape(slots, channels, count * width)


def shift_right(x, amount, bits):
    for b in range(bits):
        step = 1 << b
        moved = jnp.concatenate(
            [jnp.zeros(x.shape[:-1] + (step,), x.dtype), x[..., :-step]], axis=-1
        )
        x = jnp.where(((amount >> b) & 1)[:, None, None] == 1, moved, x)
    return x


def atom_rows(projector_full, coupling, atom_start, atom_count, ext):
    slots, channels, support = projector_full.shape
    first = jnp.clip(atom_start.astype(jnp.int32), 0, ext - support)
    padded = jnp.concatenate(
        [projector_full, jnp.zeros((slots, channels, ext - support), projector_full.dtype)], axis=-1
    )
    placed = shift_right(padded, first, (ext - support).bit_length())
    live = jnp.arange(slots, dtype=jnp.int32)[:, None] < atom_count.astype(jnp.int32)[None, :]
    weights = coupling * live.astype(jnp.float32)
    return placed.reshape(slots * channels, ext), weights.reshape(slots * channels)


def cell_maps(cell_matrix, connectivity, ext):
    cells, nodes, _ = cell_matrix.shape
    rows = jnp.arange(ext, dtype=connectivity.dtype)
    onehot = (connectivity[:, :, None] == rows[None, None, :]).astype(jnp.float32)
    moved = jnp.stack(
        [jnp.dot(cell_matrix[c], onehot[c], precision=lax.Precision.HIGH) for c in range(cells)]
    )
    return onehot.reshape(cells * nodes, ext), moved.reshape(cells * nodes, ext)


def scatter_rows(onehot, values):
    return lax.dot_general(
        onehot, values, (((0,), (0,)), ((), ())), precision=lax.Precision.HIGH
    )


def on_device(
    wavefunctions, cell_matrix, connectivity, projector, coupling, atom_start, atom_count
):
    own = wavefunctions.shape[0]
    g = GHOST
    ext = own + 2 * g
    count = lax.axis_size("dom")
    me = lax.axis_index("dom")

    low = from_left(wavefunctions[own - g :], "dom")
    high = from_right(wavefunctions[:g], "dom")
    extended = jnp.concatenate([low, wavefunctions, high], axis=0)

    placed, weights = atom_rows(gather_band(projector), coupling, atom_start, atom_count, ext)
    onehot, moved = cell_maps(cell_matrix, connectivity, ext)

    coefficients = jnp.dot(placed, extended, precision=highest) * weights[:, None]
    local = jnp.dot(moved, extended, precision=lax.Precision.HIGH)
    first = scatter_rows(onehot, local) + jnp.dot(placed.T, coefficients, precision=highest)

    moved, first = lax.optimization_barrier((moved, first))
    operator = scatter_rows(onehot, moved) + jnp.dot(
        (placed * weights[:, None]).T, placed, precision=highest
    )
    left_sums = from_left(first[ext - 2 * g :], "dom")
    right_sums = from_right(first[: 2 * g], "dom")
    zeros_side = jnp.zeros((ext - 2 * g, first.shape[1]), jnp.float32)
    first_image = (
        first
        + jnp.concatenate([left_sums, zeros_side], axis=0)
        + jnp.concatenate([zeros_side, right_sums], axis=0)
    )
    step_ext = (first_image - filter_center * extended) / filter_half
    row = lax.broadcasted_iota(jnp.int32, (ext, 1), 0)
    keep = jnp.logical_and(
        jnp.logical_or(row >= g, me > 0), jnp.logical_or(row < ext - g, me < count - 1)
    )
    step_ext = jnp.where(keep, step_ext, 0.0)
    step_one = step_ext[g : g + own]

    edges = jnp.concatenate([operator[:g], operator[ext - g :]], axis=0)
    second_edges = jnp.dot(edges, step_ext, precision=lax.Precision.HIGH)
    from_before = from_left(second_edges[g:], "dom")
    from_after = from_right(second_edges[:g], "dom")
    owned = jnp.dot(operator[g : g + own], step_ext, precision=lax.Precision.HIGH)
    zeros_own = jnp.zeros((own - g, owned.shape[1]), jnp.float32)
    second_image = (
        owned
        + jnp.concatenate([from_before, zeros_own], axis=0)
        + jnp.concatenate([zeros_own, from_after], axis=0)
    )
    filtered = 2.0 * (second_image - filter_center * step_one) / filter_half - wavefunctions
    return filtered


def solution(mesh):
    return jax.shard_map(
        on_device,
        mesh=mesh,
        in_specs=(
            P("dom", "band"),
            P("dom", None, None),
            P("dom", None),
            P("dom", None, "band"),
            P("dom", None),
            P("dom"),
            P("dom"),
        ),
        out_specs=P("dom", "band"),
        check_vma=False,
    )
```

```python
import jax
import jax.numpy as jnp
from jax import lax
from jax.sharding import PartitionSpec as P

GHOST = 128


filter_center = 0.25
filter_half = 2.0
highest = lax.Precision.HIGHEST


def from_left(x, axis):
    count = lax.axis_size(axis)
    return lax.ppermute(x, axis, [(i, i + 1) for i in range(count - 1)])


def from_right(x, axis):
    count = lax.axis_size(axis)
    return lax.ppermute(x, axis, [(i + 1, i) for i in range(count - 1)])


def gather_band(piece):
    count = lax.axis_size("band")
    me = lax.axis_index("band")
    pieces = [piece]
    for k in range(1, count):
        pieces.append(
            lax.ppermute(piece, "band", [(i, (i + k) % count) for i in range(count)])
        )
    stacked = jnp.stack(pieces)
    order = (me - jnp.arange(count)) % count
    ordered = jnp.take(stacked, order, axis=0)
    slots, channels, width = piece.shape
    return ordered.transpose(1, 2, 0, 3).reshape(slots, channels, count * width)


def shift_right(x, amount, bits):
    for b in range(bits):
        step = 1 << b
        moved = jnp.concatenate(
            [jnp.zeros(x.shape[:-1] + (step,), x.dtype), x[..., :-step]], axis=-1
        )
        x = jnp.where(((amount >> b) & 1)[:, None, None] == 1, moved, x)
    return x


def atom_rows(projector_full, coupling, atom_start, atom_count, ext):
    slots, channels, support = projector_full.shape
    first = jnp.clip(atom_start.astype(jnp.int32), 0, ext - support)
    padded = jnp.concatenate(
        [projector_full, jnp.zeros((slots, channels, ext - support), projector_full.dtype)], axis=-1
    )
    placed = shift_right(padded, first, (ext - support).bit_length())
    live = jnp.arange(slots, dtype=jnp.int32)[:, None] < atom_count.astype(jnp.int32)[None, :]
    weights = coupling * live.astype(jnp.float32)
    return placed.reshape(slots * channels, ext), weights.reshape(slots * channels)


def cell_maps(cell_matrix, connectivity, ext):
    cells, nodes, _ = cell_matrix.shape
    rows = jnp.arange(ext, dtype=connectivity.dtype)
    onehot = (connectivity[:, :, None] == rows[None, None, :]).astype(jnp.float32)
    moved = jnp.einsum("cij,cjq->ciq", cell_matrix, onehot, precision=lax.Precision.HIGH)
    return onehot.reshape(cells * nodes, ext), moved.reshape(cells * nodes, ext)


def scatter_rows(onehot, values):
    return lax.dot_general(
        onehot, values, (((0,), (0,)), ((), ())), precision=lax.Precision.HIGH
    )


def on_device(
    wavefunctions, cell_matrix, connectivity, projector, coupling, atom_start, atom_count
):
    own = wavefunctions.shape[0]
    g = GHOST
    ext = own + 2 * g
    count = lax.axis_size("dom")
    me = lax.axis_index("dom")

    low = from_left(wavefunctions[own - g :], "dom")
    high = from_right(wavefunctions[:g], "dom")
    extended = jnp.concatenate([low, wavefunctions, high], axis=0)

    placed, weights = atom_rows(gather_band(projector), coupling, atom_start, atom_count, ext)
    onehot, moved = cell_maps(cell_matrix, connectivity, ext)

    coefficients = jnp.dot(placed, extended, precision=highest) * weights[:, None]
    local = jnp.dot(moved, extended, precision=lax.Precision.HIGH)
    first = scatter_rows(onehot, local) + jnp.dot(placed.T, coefficients, precision=highest)

    moved, first = lax.optimization_barrier((moved, first))
    operator = scatter_rows(onehot, moved) + jnp.dot(
        (placed * weights[:, None]).T, placed, precision=highest
    )
    left_sums = from_left(first[ext - 2 * g :], "dom")
    right_sums = from_right(first[: 2 * g], "dom")
    zeros_side = jnp.zeros((ext - 2 * g, first.shape[1]), jnp.float32)
    first_image = (
        first
        + jnp.concatenate([left_sums, zeros_side], axis=0)
        + jnp.concatenate([zeros_side, right_sums], axis=0)
    )
    step_ext = (first_image - filter_center * extended) / filter_half
    row = lax.broadcasted_iota(jnp.int32, (ext, 1), 0)
    keep = jnp.logical_and(
        jnp.logical_or(row >= g, me > 0), jnp.logical_or(row < ext - g, me < count - 1)
    )
    step_ext = jnp.where(keep, step_ext, 0.0)
    step_one = step_ext[g : g + own]

    edges = jnp.concatenate([operator[:g], operator[ext - g :]], axis=0)
    second_edges = jnp.dot(edges, step_ext, precision=lax.Precision.HIGH)
    from_before = from_left(second_edges[g:], "dom")
    from_after = from_right(second_edges[:g], "dom")
    owned = lax.optimization_barrier(
        jnp.dot(operator[g : g + own], step_ext, precision=lax.Precision.HIGH)
    )
    zeros_own = jnp.zeros((own - g, owned.shape[1]), jnp.float32)
    second_image = (
        owned
        + jnp.concatenate([from_before, zeros_own], axis=0)
        + jnp.concatenate([zeros_own, from_after], axis=0)
    )
    filtered = 2.0 * (second_image - filter_center * step_one) / filter_half - wavefunctions
    return filtered


def solution(mesh):
    return jax.shard_map(
        on_device,
        mesh=mesh,
        in_specs=(
            P("dom", "band"),
            P("dom", None, None),
            P("dom", None),
            P("dom", None, "band"),
            P("dom", None),
            P("dom"),
            P("dom"),
        ),
        out_specs=P("dom", "band"),
        check_vma=False,
    )
```

```python
import jax
import jax.numpy as jnp
from jax import lax
from jax.sharding import PartitionSpec as P

GHOST = 128


filter_center = 0.25
filter_half = 2.0
highest = lax.Precision.HIGHEST


def from_left(x, axis):
    count = lax.axis_size(axis)
    return lax.ppermute(x, axis, [(i, i + 1) for i in range(count - 1)])


def from_right(x, axis):
    count = lax.axis_size(axis)
    return lax.ppermute(x, axis, [(i + 1, i) for i in range(count - 1)])


def gather_band(piece):
    count = lax.axis_size("band")
    me = lax.axis_index("band")
    pieces = [piece]
    for k in range(1, count):
        pieces.append(
            lax.ppermute(piece, "band", [(i, (i + k) % count) for i in range(count)])
        )
    stacked = jnp.stack(pieces)
    order = (me - jnp.arange(count)) % count
    ordered = jnp.take(stacked, order, axis=0)
    slots, channels, width = piece.shape
    return ordered.transpose(1, 2, 0, 3).reshape(slots, channels, count * width)


def shift_right(x, amount, bits):
    for b in range(bits):
        step = 1 << b
        moved = jnp.concatenate(
            [jnp.zeros(x.shape[:-1] + (step,), x.dtype), x[..., :-step]], axis=-1
        )
        x = jnp.where(((amount >> b) & 1)[:, None, None] == 1, moved, x)
    return x


def atom_rows(projector_full, coupling, atom_start, atom_count, ext):
    slots, channels, support = projector_full.shape
    first = jnp.clip(atom_start.astype(jnp.int32), 0, ext - support)
    padded = jnp.concatenate(
        [projector_full, jnp.zeros((slots, channels, ext - support), projector_full.dtype)], axis=-1
    )
    placed = shift_right(padded, first, (ext - support).bit_length())
    live = jnp.arange(slots, dtype=jnp.int32)[:, None] < atom_count.astype(jnp.int32)[None, :]
    weights = coupling * live.astype(jnp.float32)
    return placed.reshape(slots * channels, ext), weights.reshape(slots * channels)


def cell_rows(connectivity, ext):
    cells, nodes = connectivity.shape
    rows = jnp.arange(ext, dtype=connectivity.dtype)
    onehot = (connectivity[:, :, None] == rows[None, None, :]).astype(jnp.float32)
    return onehot.reshape(cells * nodes, ext)


def scatter_rows(onehot, values):
    return lax.dot_general(
        onehot, values, (((0,), (0,)), ((), ())), precision=lax.Precision.HIGH
    )


def on_device(
    wavefunctions, cell_matrix, connectivity, projector, coupling, atom_start, atom_count
):
    own = wavefunctions.shape[0]
    g = GHOST
    ext = own + 2 * g
    count = lax.axis_size("dom")
    me = lax.axis_index("dom")

    low = from_left(wavefunctions[own - g :], "dom")
    high = from_right(wavefunctions[:g], "dom")
    extended = jnp.concatenate([low, wavefunctions, high], axis=0)

    placed, weights = atom_rows(gather_band(projector), coupling, atom_start, atom_count, ext)
    onehot = cell_rows(connectivity, ext)
    cells, nodes, _ = cell_matrix.shape
    high = lax.Precision.HIGH

    coefficients = jnp.dot(placed, extended, precision=highest) * weights[:, None]
    gathered = jnp.dot(onehot, extended, precision=high).reshape(cells, nodes, -1)
    local = jnp.einsum("cij,cjb->cib", cell_matrix, gathered, precision=high)
    first = scatter_rows(onehot, local.reshape(cells * nodes, -1)) + jnp.dot(
        placed.T, coefficients, precision=highest
    )

    matrices, first = lax.optimization_barrier((cell_matrix, first))
    moved = jnp.einsum(
        "cij,cjq->ciq", matrices, onehot.reshape(cells, nodes, ext), precision=high
    )
    operator = scatter_rows(onehot, moved.reshape(cells * nodes, ext)) + jnp.dot(
        (placed * weights[:, None]).T, placed, precision=highest
    )
    left_sums = from_left(first[ext - 2 * g :], "dom")
    right_sums = from_right(first[: 2 * g], "dom")
    zeros_side = jnp.zeros((ext - 2 * g, first.shape[1]), jnp.float32)
    first_image = (
        first
        + jnp.concatenate([left_sums, zeros_side], axis=0)
        + jnp.concatenate([zeros_side, right_sums], axis=0)
    )
    step_ext = (first_image - filter_center * extended) / filter_half
    row = lax.broadcasted_iota(jnp.int32, (ext, 1), 0)
    keep = jnp.logical_and(
        jnp.logical_or(row >= g, me > 0), jnp.logical_or(row < ext - g, me < count - 1)
    )
    step_ext = jnp.where(keep, step_ext, 0.0)
    step_one = step_ext[g : g + own]

    edges = jnp.concatenate([operator[:g], operator[ext - g :]], axis=0)
    second_edges = jnp.dot(edges, step_ext, precision=lax.Precision.HIGH)
    from_before = from_left(second_edges[g:], "dom")
    from_after = from_right(second_edges[:g], "dom")
    owned = lax.optimization_barrier(
        jnp.dot(operator[g : g + own], step_ext, precision=lax.Precision.HIGH)
    )
    zeros_own = jnp.zeros((own - g, owned.shape[1]), jnp.float32)
    second_image = (
        owned
        + jnp.concatenate([from_before, zeros_own], axis=0)
        + jnp.concatenate([zeros_own, from_after], axis=0)
    )
    filtered = 2.0 * (second_image - filter_center * step_one) / filter_half - wavefunctions
    return filtered


def solution(mesh):
    return jax.shard_map(
        on_device,
        mesh=mesh,
        in_specs=(
            P("dom", "band"),
            P("dom", None, None),
            P("dom", None),
            P("dom", None, "band"),
            P("dom", None),
            P("dom"),
            P("dom"),
        ),
        out_specs=P("dom", "band"),
        check_vma=False,
    )
```

```python
import jax
import jax.numpy as jnp
from jax import lax
from jax.sharding import PartitionSpec as P

GHOST = 128


filter_center = 0.25
filter_half = 2.0
highest = lax.Precision.HIGHEST


def from_left(x, axis):
    count = lax.axis_size(axis)
    return lax.ppermute(x, axis, [(i, i + 1) for i in range(count - 1)])


def from_right(x, axis):
    count = lax.axis_size(axis)
    return lax.ppermute(x, axis, [(i + 1, i) for i in range(count - 1)])


def gather_band(piece):
    count = lax.axis_size("band")
    total = piece
    for k in range(1, count):
        total = total + lax.ppermute(piece, "band", [(i, (i + k) % count) for i in range(count)])
    return total


def shift_right(x, amount, bits):
    for b in range(bits):
        step = 1 << b
        moved = jnp.concatenate(
            [jnp.zeros(x.shape[:-1] + (step,), x.dtype), x[..., :-step]], axis=-1
        )
        x = jnp.where(((amount >> b) & 1)[:, None, None] == 1, moved, x)
    return x


def atom_rows(projector, coupling, atom_start, atom_count, ext):
    slots, channels, width = projector.shape
    support = width * lax.axis_size("band")
    first = jnp.clip(atom_start.astype(jnp.int32), 0, ext - support)
    offset = first + lax.axis_index("band").astype(jnp.int32) * width
    padded = jnp.concatenate(
        [projector, jnp.zeros((slots, channels, ext - width), projector.dtype)], axis=-1
    )
    placed = gather_band(shift_right(padded, offset, (ext - width).bit_length()))
    live = jnp.arange(slots, dtype=jnp.int32)[:, None] < atom_count.astype(jnp.int32)[None, :]
    weights = coupling * live.astype(jnp.float32)
    return placed.reshape(slots * channels, ext), weights.reshape(slots * channels)


def cell_rows(connectivity, ext):
    cells, nodes = connectivity.shape
    rows = jnp.arange(ext, dtype=connectivity.dtype)
    onehot = (connectivity[:, :, None] == rows[None, None, :]).astype(jnp.float32)
    return onehot.reshape(cells * nodes, ext)


def scatter_rows(onehot, values):
    return lax.dot_general(
        onehot, values, (((0,), (0,)), ((), ())), precision=lax.Precision.HIGH
    )


def on_device(
    wavefunctions, cell_matrix, connectivity, projector, coupling, atom_start, atom_count
):
    own = wavefunctions.shape[0]
    g = GHOST
    ext = own + 2 * g
    count = lax.axis_size("dom")
    me = lax.axis_index("dom")

    low = from_left(wavefunctions[own - g :], "dom")
    high = from_right(wavefunctions[:g], "dom")
    extended = jnp.concatenate([low, wavefunctions, high], axis=0)

    placed, weights = atom_rows(projector, coupling, atom_start, atom_count, ext)
    onehot = cell_rows(connectivity, ext)
    cells, nodes, _ = cell_matrix.shape
    high = lax.Precision.HIGH

    coefficients = jnp.dot(placed, extended, precision=highest) * weights[:, None]
    gathered = jnp.dot(onehot, extended, precision=high).reshape(cells, nodes, -1)
    local = jnp.einsum("cij,cjb->cib", cell_matrix, gathered, precision=high)
    first = scatter_rows(onehot, local.reshape(cells * nodes, -1)) + jnp.dot(
        placed.T, coefficients, precision=highest
    )

    matrices, first = lax.optimization_barrier((cell_matrix, first))
    moved = jnp.einsum(
        "cij,cjq->ciq", matrices, onehot.reshape(cells, nodes, ext), precision=high
    )
    operator = scatter_rows(onehot, moved.reshape(cells * nodes, ext)) + jnp.dot(
        (placed * weights[:, None]).T, placed, precision=highest
    )
    left_sums = from_left(first[ext - 2 * g :], "dom")
    right_sums = from_right(first[: 2 * g], "dom")
    zeros_side = jnp.zeros((ext - 2 * g, first.shape[1]), jnp.float32)
    first_image = (
        first
        + jnp.concatenate([left_sums, zeros_side], axis=0)
        + jnp.concatenate([zeros_side, right_sums], axis=0)
    )
    step_ext = (first_image - filter_center * extended) / filter_half
    row = lax.broadcasted_iota(jnp.int32, (ext, 1), 0)
    keep = jnp.logical_and(
        jnp.logical_or(row >= g, me > 0), jnp.logical_or(row < ext - g, me < count - 1)
    )
    step_ext = jnp.where(keep, step_ext, 0.0)
    step_one = step_ext[g : g + own]

    edges = jnp.concatenate([operator[:g], operator[ext - g :]], axis=0)
    second_edges = jnp.dot(edges, step_ext, precision=lax.Precision.HIGH)
    from_before = from_left(second_edges[g:], "dom")
    from_after = from_right(second_edges[:g], "dom")
    owned = lax.optimization_barrier(
        jnp.dot(operator[g : g + own], step_ext, precision=lax.Precision.HIGH)
    )
    zeros_own = jnp.zeros((own - g, owned.shape[1]), jnp.float32)
    second_image = (
        owned
        + jnp.concatenate([from_before, zeros_own], axis=0)
        + jnp.concatenate([zeros_own, from_after], axis=0)
    )
    filtered = 2.0 * (second_image - filter_center * step_one) / filter_half - wavefunctions
    return filtered


def solution(mesh):
    return jax.shard_map(
        on_device,
        mesh=mesh,
        in_specs=(
            P("dom", "band"),
            P("dom", None, None),
            P("dom", None),
            P("dom", None, "band"),
            P("dom", None),
            P("dom"),
            P("dom"),
        ),
        out_specs=P("dom", "band"),
        check_vma=False,
    )
```

```python
import jax
import jax.numpy as jnp
from jax import lax
from jax.sharding import PartitionSpec as P

GHOST = 128


filter_center = 0.25
filter_half = 2.0
highest = lax.Precision.HIGHEST


def from_left(x, axis):
    count = lax.axis_size(axis)
    return lax.ppermute(x, axis, [(i, i + 1) for i in range(count - 1)])


def from_right(x, axis):
    count = lax.axis_size(axis)
    return lax.ppermute(x, axis, [(i + 1, i) for i in range(count - 1)])


def gather_band(piece):
    return lax.all_gather(piece, "band", axis=2, tiled=True)


def shift_right(x, amount, bits):
    for b in range(bits):
        step = 1 << b
        moved = jnp.concatenate(
            [jnp.zeros(x.shape[:-1] + (step,), x.dtype), x[..., :-step]], axis=-1
        )
        x = jnp.where(((amount >> b) & 1)[:, None, None] == 1, moved, x)
    return x


def atom_rows(projector_full, coupling, atom_start, atom_count, ext):
    slots, channels, support = projector_full.shape
    first = jnp.clip(atom_start.astype(jnp.int32), 0, ext - support)
    padded = jnp.concatenate(
        [projector_full, jnp.zeros((slots, channels, ext - support), projector_full.dtype)], axis=-1
    )
    placed = shift_right(padded, first, (ext - support).bit_length())
    live = jnp.arange(slots, dtype=jnp.int32)[:, None] < atom_count.astype(jnp.int32)[None, :]
    weights = coupling * live.astype(jnp.float32)
    return placed.reshape(slots * channels, ext), weights.reshape(slots * channels)


def cell_rows(connectivity, ext):
    cells, nodes = connectivity.shape
    rows = jnp.arange(ext, dtype=connectivity.dtype)
    onehot = (connectivity[:, :, None] == rows[None, None, :]).astype(jnp.float32)
    return onehot.reshape(cells * nodes, ext)


def scatter_rows(onehot, values):
    return lax.dot_general(
        onehot, values, (((0,), (0,)), ((), ())), precision=lax.Precision.HIGH
    )


def on_device(
    wavefunctions, cell_matrix, connectivity, projector, coupling, atom_start, atom_count
):
    own = wavefunctions.shape[0]
    g = GHOST
    ext = own + 2 * g
    count = lax.axis_size("dom")
    me = lax.axis_index("dom")

    low = from_left(wavefunctions[own - g :], "dom")
    high = from_right(wavefunctions[:g], "dom")
    extended = jnp.concatenate([low, wavefunctions, high], axis=0)

    placed, weights = atom_rows(gather_band(projector), coupling, atom_start, atom_count, ext)
    onehot = cell_rows(connectivity, ext)
    cells, nodes, _ = cell_matrix.shape
    high = lax.Precision.HIGH

    coefficients = jnp.dot(placed, extended, precision=high) * weights[:, None]
    gathered = jnp.dot(onehot, extended, precision=high).reshape(cells, nodes, -1)
    local = jnp.einsum("cij,cjb->cib", cell_matrix, gathered, precision=high)
    first = scatter_rows(onehot, local.reshape(cells * nodes, -1)) + jnp.dot(
        placed.T, coefficients, precision=high
    )

    matrices, first = lax.optimization_barrier((cell_matrix, first))
    moved = jnp.einsum(
        "cij,cjq->ciq", matrices, onehot.reshape(cells, nodes, ext), precision=high
    )
    operator = scatter_rows(onehot, moved.reshape(cells * nodes, ext)) + jnp.dot(
        (placed * weights[:, None]).T, placed, precision=highest
    )
    left_sums = from_left(first[ext - 2 * g :], "dom")
    right_sums = from_right(first[: 2 * g], "dom")
    zeros_side = jnp.zeros((ext - 2 * g, first.shape[1]), jnp.float32)
    first_image = (
        first
        + jnp.concatenate([left_sums, zeros_side], axis=0)
        + jnp.concatenate([zeros_side, right_sums], axis=0)
    )
    step_ext = (first_image - filter_center * extended) / filter_half
    row = lax.broadcasted_iota(jnp.int32, (ext, 1), 0)
    keep = jnp.logical_and(
        jnp.logical_or(row >= g, me > 0), jnp.logical_or(row < ext - g, me < count - 1)
    )
    step_ext = jnp.where(keep, step_ext, 0.0)
    step_one = step_ext[g : g + own]

    edges = jnp.concatenate([operator[:g], operator[ext - g :]], axis=0)
    second_edges = jnp.dot(edges, step_ext, precision=lax.Precision.HIGH)
    from_before = from_left(second_edges[g:], "dom")
    from_after = from_right(second_edges[:g], "dom")
    owned = lax.optimization_barrier(
        jnp.dot(operator[g : g + own], step_ext, precision=lax.Precision.HIGH)
    )
    zeros_own = jnp.zeros((own - g, owned.shape[1]), jnp.float32)
    second_image = (
        owned
        + jnp.concatenate([from_before, zeros_own], axis=0)
        + jnp.concatenate([zeros_own, from_after], axis=0)
    )
    filtered = 2.0 * (second_image - filter_center * step_one) / filter_half - wavefunctions
    return filtered


def solution(mesh):
    return jax.shard_map(
        on_device,
        mesh=mesh,
        in_specs=(
            P("dom", "band"),
            P("dom", None, None),
            P("dom", None),
            P("dom", None, "band"),
            P("dom", None),
            P("dom"),
            P("dom"),
        ),
        out_specs=P("dom", "band"),
        check_vma=False,
    )
```

```python
import jax
import jax.numpy as jnp
from jax import lax
from jax.sharding import PartitionSpec as P

GHOST = 128


filter_center = 0.25
filter_half = 2.0
highest = lax.Precision.HIGHEST


def from_left(x, axis):
    count = lax.axis_size(axis)
    return lax.ppermute(x, axis, [(i, i + 1) for i in range(count - 1)])


def from_right(x, axis):
    count = lax.axis_size(axis)
    return lax.ppermute(x, axis, [(i + 1, i) for i in range(count - 1)])


def gather_band(piece):
    count = lax.axis_size("band")
    me = lax.axis_index("band")
    pieces = [piece]
    for k in range(1, count):
        pieces.append(
            lax.ppermute(piece, "band", [(i, (i + k) % count) for i in range(count)])
        )
    stacked = jnp.stack(pieces)
    order = (me - jnp.arange(count)) % count
    ordered = jnp.take(stacked, order, axis=0)
    slots, channels, width = piece.shape
    return ordered.transpose(1, 2, 0, 3).reshape(slots, channels, count * width)


def shift_right(x, amount, bits):
    for b in range(bits):
        step = 1 << b
        moved = jnp.concatenate(
            [jnp.zeros(x.shape[:-1] + (step,), x.dtype), x[..., :-step]], axis=-1
        )
        x = jnp.where(((amount >> b) & 1)[:, None, None] == 1, moved, x)
    return x


def atom_rows(projector_full, coupling, atom_start, atom_count, ext):
    slots, channels, support = projector_full.shape
    first = jnp.clip(atom_start.astype(jnp.int32), 0, ext - support)
    padded = jnp.concatenate(
        [projector_full, jnp.zeros((slots, channels, ext - support), projector_full.dtype)], axis=-1
    )
    placed = shift_right(padded, first, (ext - support).bit_length())
    live = jnp.arange(slots, dtype=jnp.int32)[:, None] < atom_count.astype(jnp.int32)[None, :]
    weights = coupling * live.astype(jnp.float32)
    return placed.reshape(slots * channels, ext), weights.reshape(slots * channels)


def cell_rows(connectivity, ext):
    cells, nodes = connectivity.shape
    rows = jnp.arange(ext, dtype=connectivity.dtype)
    onehot = (connectivity[:, :, None] == rows[None, None, :]).astype(jnp.float32)
    return onehot.reshape(cells * nodes, ext)


def scatter_rows(onehot, values):
    return lax.dot_general(
        onehot, values, (((0,), (0,)), ((), ())), precision=lax.Precision.HIGH
    )


def on_device(
    wavefunctions, cell_matrix, connectivity, projector, coupling, atom_start, atom_count
):
    own = wavefunctions.shape[0]
    g = GHOST
    ext = own + 2 * g
    count = lax.axis_size("dom")
    me = lax.axis_index("dom")

    low = from_left(wavefunctions[own - g :], "dom")
    high = from_right(wavefunctions[:g], "dom")
    extended = jnp.concatenate([low, wavefunctions, high], axis=0)

    placed, weights = atom_rows(gather_band(projector), coupling, atom_start, atom_count, ext)
    onehot = cell_rows(connectivity, ext)
    cells, nodes, _ = cell_matrix.shape
    high = lax.Precision.HIGH

    coefficients = jnp.dot(placed, extended, precision=highest) * weights[:, None]
    gathered = jnp.dot(onehot, extended, precision=high).reshape(cells, nodes, -1)
    local = jnp.einsum("cij,cjb->cib", cell_matrix, gathered, precision=high)
    first = scatter_rows(onehot, local.reshape(cells * nodes, -1)) + jnp.dot(
        placed.T, coefficients, precision=highest
    )

    matrices, placed_late, weights_late, first = lax.optimization_barrier(
        (cell_matrix, placed, weights, first)
    )
    moved = jnp.einsum(
        "cij,cjq->ciq", matrices, onehot.reshape(cells, nodes, ext), precision=high
    )
    operator = scatter_rows(onehot, moved.reshape(cells * nodes, ext)) + jnp.dot(
        (placed_late * weights_late[:, None]).T, placed_late, precision=highest
    )
    left_sums = from_left(first[ext - 2 * g :], "dom")
    right_sums = from_right(first[: 2 * g], "dom")
    zeros_side = jnp.zeros((ext - 2 * g, first.shape[1]), jnp.float32)
    first_image = (
        first
        + jnp.concatenate([left_sums, zeros_side], axis=0)
        + jnp.concatenate([zeros_side, right_sums], axis=0)
    )
    step_ext = (first_image - filter_center * extended) / filter_half
    row = lax.broadcasted_iota(jnp.int32, (ext, 1), 0)
    keep = jnp.logical_and(
        jnp.logical_or(row >= g, me > 0), jnp.logical_or(row < ext - g, me < count - 1)
    )
    step_ext = jnp.where(keep, step_ext, 0.0)
    step_one = step_ext[g : g + own]

    edges = jnp.concatenate([operator[:g], operator[ext - g :]], axis=0)
    second_edges = jnp.dot(edges, step_ext, precision=lax.Precision.HIGH)
    from_before = from_left(second_edges[g:], "dom")
    from_after = from_right(second_edges[:g], "dom")
    owned = lax.optimization_barrier(
        jnp.dot(operator[g : g + own], step_ext, precision=lax.Precision.HIGH)
    )
    zeros_own = jnp.zeros((own - g, owned.shape[1]), jnp.float32)
    second_image = (
        owned
        + jnp.concatenate([from_before, zeros_own], axis=0)
        + jnp.concatenate([zeros_own, from_after], axis=0)
    )
    filtered = 2.0 * (second_image - filter_center * step_one) / filter_half - wavefunctions
    return filtered


def solution(mesh):
    return jax.shard_map(
        on_device,
        mesh=mesh,
        in_specs=(
            P("dom", "band"),
            P("dom", None, None),
            P("dom", None),
            P("dom", None, "band"),
            P("dom", None),
            P("dom"),
            P("dom"),
        ),
        out_specs=P("dom", "band"),
        check_vma=False,
    )
```

```python
import jax
import jax.numpy as jnp
from jax import lax
from jax.sharding import PartitionSpec as P

GHOST = 128


filter_center = 0.25
filter_half = 2.0
highest = lax.Precision.HIGHEST


def from_left(x, axis):
    count = lax.axis_size(axis)
    return lax.ppermute(x, axis, [(i, i + 1) for i in range(count - 1)])


def from_right(x, axis):
    count = lax.axis_size(axis)
    return lax.ppermute(x, axis, [(i + 1, i) for i in range(count - 1)])


def gather_band(piece):
    count = lax.axis_size("band")
    me = lax.axis_index("band")
    pieces = [piece]
    for k in range(1, count):
        pieces.append(
            lax.ppermute(piece, "band", [(i, (i + k) % count) for i in range(count)])
        )
    ordered = []
    for src in range(count):
        shift = (me - src) % count
        block = jnp.zeros_like(piece)
        for k in range(count):
            block = block + jnp.where(shift == k, pieces[k], 0.0)
        ordered.append(block)
    ordered = jnp.stack(ordered)
    slots, channels, width = piece.shape
    return ordered.transpose(1, 2, 0, 3).reshape(slots, channels, count * width)


def shift_right(x, amount, bits):
    for b in range(bits):
        step = 1 << b
        moved = jnp.concatenate(
            [jnp.zeros(x.shape[:-1] + (step,), x.dtype), x[..., :-step]], axis=-1
        )
        x = jnp.where(((amount >> b) & 1)[:, None, None] == 1, moved, x)
    return x


def atom_rows(projector_full, coupling, atom_start, atom_count, ext):
    slots, channels, support = projector_full.shape
    first = jnp.clip(atom_start.astype(jnp.int32), 0, ext - support)
    padded = jnp.concatenate(
        [projector_full, jnp.zeros((slots, channels, ext - support), projector_full.dtype)], axis=-1
    )
    placed = shift_right(padded, first, (ext - support).bit_length())
    live = jnp.arange(slots, dtype=jnp.int32)[:, None] < atom_count.astype(jnp.int32)[None, :]
    weights = coupling * live.astype(jnp.float32)
    return placed.reshape(slots * channels, ext), weights.reshape(slots * channels)


def cell_rows(connectivity, ext):
    cells, nodes = connectivity.shape
    rows = jnp.arange(ext, dtype=connectivity.dtype)
    onehot = (connectivity[:, :, None] == rows[None, None, :]).astype(jnp.float32)
    return onehot.reshape(cells * nodes, ext)


def scatter_rows(onehot, values):
    return lax.dot_general(
        onehot, values, (((0,), (0,)), ((), ())), precision=lax.Precision.HIGH
    )


def on_device(
    wavefunctions, cell_matrix, connectivity, projector, coupling, atom_start, atom_count
):
    own = wavefunctions.shape[0]
    g = GHOST
    ext = own + 2 * g
    count = lax.axis_size("dom")
    me = lax.axis_index("dom")

    low = from_left(wavefunctions[own - g :], "dom")
    high = from_right(wavefunctions[:g], "dom")
    extended = jnp.concatenate([low, wavefunctions, high], axis=0)

    placed, weights = atom_rows(gather_band(projector), coupling, atom_start, atom_count, ext)
    onehot = cell_rows(connectivity, ext)
    cells, nodes, _ = cell_matrix.shape
    high = lax.Precision.HIGH

    coefficients = jnp.dot(placed, extended, precision=highest) * weights[:, None]
    gathered = jnp.dot(onehot, extended, precision=high).reshape(cells, nodes, -1)
    local = jnp.einsum("cij,cjb->cib", cell_matrix, gathered, precision=high)
    first = scatter_rows(onehot, local.reshape(cells * nodes, -1)) + jnp.dot(
        placed.T, coefficients, precision=highest
    )

    matrices, placed_late, weights_late, first = lax.optimization_barrier(
        (cell_matrix, placed, weights, first)
    )
    moved = jnp.einsum(
        "cij,cjq->ciq", matrices, onehot.reshape(cells, nodes, ext), precision=high
    )
    operator = scatter_rows(onehot, moved.reshape(cells * nodes, ext)) + jnp.dot(
        (placed_late * weights_late[:, None]).T, placed_late, precision=highest
    )
    left_sums = from_left(first[ext - 2 * g :], "dom")
    right_sums = from_right(first[: 2 * g], "dom")
    zeros_side = jnp.zeros((ext - 2 * g, first.shape[1]), jnp.float32)
    first_image = (
        first
        + jnp.concatenate([left_sums, zeros_side], axis=0)
        + jnp.concatenate([zeros_side, right_sums], axis=0)
    )
    step_ext = (first_image - filter_center * extended) / filter_half
    row = lax.broadcasted_iota(jnp.int32, (ext, 1), 0)
    keep = jnp.logical_and(
        jnp.logical_or(row >= g, me > 0), jnp.logical_or(row < ext - g, me < count - 1)
    )
    step_ext = jnp.where(keep, step_ext, 0.0)
    step_one = step_ext[g : g + own]

    edges = jnp.concatenate([operator[:g], operator[ext - g :]], axis=0)
    second_edges = jnp.dot(edges, step_ext, precision=lax.Precision.HIGH)
    from_before = from_left(second_edges[g:], "dom")
    from_after = from_right(second_edges[:g], "dom")
    owned = lax.optimization_barrier(
        jnp.dot(operator[g : g + own], step_ext, precision=lax.Precision.HIGH)
    )
    zeros_own = jnp.zeros((own - g, owned.shape[1]), jnp.float32)
    second_image = (
        owned
        + jnp.concatenate([from_before, zeros_own], axis=0)
        + jnp.concatenate([zeros_own, from_after], axis=0)
    )
    filtered = 2.0 * (second_image - filter_center * step_one) / filter_half - wavefunctions
    return filtered


def solution(mesh):
    return jax.shard_map(
        on_device,
        mesh=mesh,
        in_specs=(
            P("dom", "band"),
            P("dom", None, None),
            P("dom", None),
            P("dom", None, "band"),
            P("dom", None),
            P("dom"),
            P("dom"),
        ),
        out_specs=P("dom", "band"),
        check_vma=False,
    )
```

```python
import jax
import jax.numpy as jnp
from jax import lax
from jax.sharding import PartitionSpec as P

GHOST = 128


filter_center = 0.25
filter_half = 2.0
highest = lax.Precision.HIGHEST


def from_left(x, axis):
    count = lax.axis_size(axis)
    return lax.ppermute(x, axis, [(i, i + 1) for i in range(count - 1)])


def from_right(x, axis):
    count = lax.axis_size(axis)
    return lax.ppermute(x, axis, [(i + 1, i) for i in range(count - 1)])


def gather_band(piece):
    count = lax.axis_size("band")
    me = lax.axis_index("band")
    pieces = [piece]
    for k in range(1, count):
        pieces.append(
            lax.ppermute(piece, "band", [(i, (i + k) % count) for i in range(count)])
        )
    ordered = []
    for src in range(count):
        shift = (me - src) % count
        block = jnp.zeros_like(piece)
        for k in range(count):
            block = block + jnp.where(shift == k, pieces[k], 0.0)
        ordered.append(block)
    ordered = jnp.stack(ordered)
    slots, channels, width = piece.shape
    return ordered.transpose(1, 2, 0, 3).reshape(slots, channels, count * width)


def shift_right(x, amount, bits):
    for b in range(bits):
        step = 1 << b
        moved = jnp.concatenate(
            [jnp.zeros(x.shape[:-1] + (step,), x.dtype), x[..., :-step]], axis=-1
        )
        x = jnp.where(((amount >> b) & 1)[:, None, None] == 1, moved, x)
    return x


def atom_rows(projector_full, coupling, atom_start, atom_count, ext):
    slots, channels, support = projector_full.shape
    first = jnp.clip(atom_start.astype(jnp.int32), 0, ext - support)
    padded = jnp.concatenate(
        [projector_full, jnp.zeros((slots, channels, ext - support), projector_full.dtype)], axis=-1
    )
    placed = shift_right(padded, first, (ext - support).bit_length())
    return placed.reshape(slots * channels, ext), atom_weights(coupling, atom_count)


def atom_weights(coupling, atom_count):
    slots, channels = coupling.shape
    live = jnp.arange(slots, dtype=jnp.int32)[:, None] < atom_count.astype(jnp.int32)[None, :]
    return (coupling * live.astype(jnp.float32)).reshape(slots * channels)


def cell_rows(connectivity, ext):
    cells, nodes = connectivity.shape
    rows = jnp.arange(ext, dtype=connectivity.dtype)
    onehot = (connectivity[:, :, None] == rows[None, None, :]).astype(jnp.float32)
    return onehot.reshape(cells * nodes, ext)


def scatter_rows(onehot, values):
    return lax.dot_general(
        onehot, values, (((0,), (0,)), ((), ())), precision=lax.Precision.HIGH
    )


def on_device(
    wavefunctions, cell_matrix, connectivity, projector, coupling, atom_start, atom_count
):
    own = wavefunctions.shape[0]
    g = GHOST
    ext = own + 2 * g
    count = lax.axis_size("dom")
    me = lax.axis_index("dom")

    low = from_left(wavefunctions[own - g :], "dom")
    high = from_right(wavefunctions[:g], "dom")
    extended = jnp.concatenate([low, wavefunctions, high], axis=0)

    placed, weights = atom_rows(gather_band(projector), coupling, atom_start, atom_count, ext)
    onehot = cell_rows(connectivity, ext)
    cells, nodes, _ = cell_matrix.shape
    high = lax.Precision.HIGH

    coefficients = jnp.dot(placed, extended, precision=highest) * weights[:, None]
    gathered = jnp.dot(onehot, extended, precision=high).reshape(cells, nodes, -1)
    local = jnp.einsum("cij,cjb->cib", cell_matrix, gathered, precision=high)
    first = scatter_rows(onehot, local.reshape(cells * nodes, -1)) + jnp.dot(
        placed.T, coefficients, precision=highest
    )

    matrices, placed_late, coupling_late, count_late, first = lax.optimization_barrier(
        (cell_matrix, placed, coupling, atom_count, first)
    )
    weights_late = atom_weights(coupling_late, count_late)
    moved = jnp.einsum(
        "cij,cjq->ciq", matrices, onehot.reshape(cells, nodes, ext), precision=high
    )
    operator = scatter_rows(onehot, moved.reshape(cells * nodes, ext)) + jnp.dot(
        (placed_late * weights_late[:, None]).T, placed_late, precision=highest
    )
    left_sums = from_left(first[ext - 2 * g :], "dom")
    right_sums = from_right(first[: 2 * g], "dom")
    zeros_side = jnp.zeros((ext - 2 * g, first.shape[1]), jnp.float32)
    first_image = (
        first
        + jnp.concatenate([left_sums, zeros_side], axis=0)
        + jnp.concatenate([zeros_side, right_sums], axis=0)
    )
    step_ext = (first_image - filter_center * extended) / filter_half
    row = lax.broadcasted_iota(jnp.int32, (ext, 1), 0)
    keep = jnp.logical_and(
        jnp.logical_or(row >= g, me > 0), jnp.logical_or(row < ext - g, me < count - 1)
    )
    step_ext = jnp.where(keep, step_ext, 0.0)
    step_one = step_ext[g : g + own]

    edges = jnp.concatenate([operator[:g], operator[ext - g :]], axis=0)
    second_edges = jnp.dot(edges, step_ext, precision=lax.Precision.HIGH)
    from_before = from_left(second_edges[g:], "dom")
    from_after = from_right(second_edges[:g], "dom")
    owned = lax.optimization_barrier(
        jnp.dot(operator[g : g + own], step_ext, precision=lax.Precision.HIGH)
    )
    zeros_own = jnp.zeros((own - g, owned.shape[1]), jnp.float32)
    second_image = (
        owned
        + jnp.concatenate([from_before, zeros_own], axis=0)
        + jnp.concatenate([zeros_own, from_after], axis=0)
    )
    filtered = 2.0 * (second_image - filter_center * step_one) / filter_half - wavefunctions
    return filtered


def solution(mesh):
    return jax.shard_map(
        on_device,
        mesh=mesh,
        in_specs=(
            P("dom", "band"),
            P("dom", None, None),
            P("dom", None),
            P("dom", None, "band"),
            P("dom", None),
            P("dom"),
            P("dom"),
        ),
        out_specs=P("dom", "band"),
        check_vma=False,
    )
```

```python
import jax
import jax.numpy as jnp
from jax import lax
from jax.sharding import PartitionSpec as P

GHOST = 128


filter_center = 0.25
filter_half = 2.0
highest = lax.Precision.HIGHEST


def from_left(x, axis):
    count = lax.axis_size(axis)
    return lax.ppermute(x, axis, [(i, i + 1) for i in range(count - 1)])


def from_right(x, axis):
    count = lax.axis_size(axis)
    return lax.ppermute(x, axis, [(i + 1, i) for i in range(count - 1)])


def gather_band(piece):
    count = lax.axis_size("band")
    copies = jnp.broadcast_to(piece[None], (count,) + piece.shape)
    ordered = lax.all_to_all(copies, "band", 0, 0, tiled=True)
    slots, channels, width = piece.shape
    return ordered.transpose(1, 2, 0, 3).reshape(slots, channels, count * width)


def shift_right(x, amount, bits):
    for b in range(bits):
        step = 1 << b
        moved = jnp.concatenate(
            [jnp.zeros(x.shape[:-1] + (step,), x.dtype), x[..., :-step]], axis=-1
        )
        x = jnp.where(((amount >> b) & 1)[:, None, None] == 1, moved, x)
    return x


def atom_rows(projector_full, coupling, atom_start, atom_count, ext):
    slots, channels, support = projector_full.shape
    first = jnp.clip(atom_start.astype(jnp.int32), 0, ext - support)
    padded = jnp.concatenate(
        [projector_full, jnp.zeros((slots, channels, ext - support), projector_full.dtype)], axis=-1
    )
    placed = shift_right(padded, first, (ext - support).bit_length())
    live = jnp.arange(slots, dtype=jnp.int32)[:, None] < atom_count.astype(jnp.int32)[None, :]
    weights = coupling * live.astype(jnp.float32)
    return placed.reshape(slots * channels, ext), weights.reshape(slots * channels)


def cell_rows(connectivity, ext):
    cells, nodes = connectivity.shape
    rows = jnp.arange(ext, dtype=connectivity.dtype)
    onehot = (connectivity[:, :, None] == rows[None, None, :]).astype(jnp.float32)
    return onehot.reshape(cells * nodes, ext)


def scatter_rows(onehot, values):
    return lax.dot_general(
        onehot, values, (((0,), (0,)), ((), ())), precision=lax.Precision.HIGH
    )


def on_device(
    wavefunctions, cell_matrix, connectivity, projector, coupling, atom_start, atom_count
):
    own = wavefunctions.shape[0]
    g = GHOST
    ext = own + 2 * g
    count = lax.axis_size("dom")
    me = lax.axis_index("dom")

    low = from_left(wavefunctions[own - g :], "dom")
    high = from_right(wavefunctions[:g], "dom")
    extended = jnp.concatenate([low, wavefunctions, high], axis=0)

    placed, weights = atom_rows(gather_band(projector), coupling, atom_start, atom_count, ext)
    onehot = cell_rows(connectivity, ext)
    cells, nodes, _ = cell_matrix.shape
    high = lax.Precision.HIGH

    coefficients = jnp.dot(placed, extended, precision=highest) * weights[:, None]
    gathered = jnp.dot(onehot, extended, precision=high).reshape(cells, nodes, -1)
    local = jnp.einsum("cij,cjb->cib", cell_matrix, gathered, precision=high)
    first = scatter_rows(onehot, local.reshape(cells * nodes, -1)) + jnp.dot(
        placed.T, coefficients, precision=highest
    )

    matrices, placed_late, weights_late, first = lax.optimization_barrier(
        (cell_matrix, placed, weights, first)
    )
    moved = jnp.einsum(
        "cij,cjq->ciq", matrices, onehot.reshape(cells, nodes, ext), precision=high
    )
    operator = scatter_rows(onehot, moved.reshape(cells * nodes, ext)) + jnp.dot(
        (placed_late * weights_late[:, None]).T, placed_late, precision=highest
    )
    left_sums = from_left(first[ext - 2 * g :], "dom")
    right_sums = from_right(first[: 2 * g], "dom")
    zeros_side = jnp.zeros((ext - 2 * g, first.shape[1]), jnp.float32)
    first_image = (
        first
        + jnp.concatenate([left_sums, zeros_side], axis=0)
        + jnp.concatenate([zeros_side, right_sums], axis=0)
    )
    step_ext = (first_image - filter_center * extended) / filter_half
    row = lax.broadcasted_iota(jnp.int32, (ext, 1), 0)
    keep = jnp.logical_and(
        jnp.logical_or(row >= g, me > 0), jnp.logical_or(row < ext - g, me < count - 1)
    )
    step_ext = jnp.where(keep, step_ext, 0.0)
    step_one = step_ext[g : g + own]

    edges = jnp.concatenate([operator[:g], operator[ext - g :]], axis=0)
    second_edges = jnp.dot(edges, step_ext, precision=lax.Precision.HIGH)
    from_before = from_left(second_edges[g:], "dom")
    from_after = from_right(second_edges[:g], "dom")
    owned = lax.optimization_barrier(
        jnp.dot(operator[g : g + own], step_ext, precision=lax.Precision.HIGH)
    )
    zeros_own = jnp.zeros((own - g, owned.shape[1]), jnp.float32)
    second_image = (
        owned
        + jnp.concatenate([from_before, zeros_own], axis=0)
        + jnp.concatenate([zeros_own, from_after], axis=0)
    )
    filtered = 2.0 * (second_image - filter_center * step_one) / filter_half - wavefunctions
    return filtered


def solution(mesh):
    return jax.shard_map(
        on_device,
        mesh=mesh,
        in_specs=(
            P("dom", "band"),
            P("dom", None, None),
            P("dom", None),
            P("dom", None, "band"),
            P("dom", None),
            P("dom"),
            P("dom"),
        ),
        out_specs=P("dom", "band"),
        check_vma=False,
    )
```

```python
import jax
import jax.numpy as jnp
from jax import lax
from jax.sharding import PartitionSpec as P

GHOST = 128


filter_center = 0.25
filter_half = 2.0
highest = lax.Precision.HIGHEST


def from_left(x, axis):
    count = lax.axis_size(axis)
    return lax.ppermute(x, axis, [(i, i + 1) for i in range(count - 1)])


def from_right(x, axis):
    count = lax.axis_size(axis)
    return lax.ppermute(x, axis, [(i + 1, i) for i in range(count - 1)])


def gather_band(piece):
    count = lax.axis_size("band")
    me = lax.axis_index("band")
    pieces = [piece]
    for k in range(1, count):
        pieces.append(
            lax.ppermute(piece, "band", [(i, (i + k) % count) for i in range(count)])
        )
    stacked = jnp.stack(pieces)
    order = (me - jnp.arange(count)) % count
    ordered = jnp.take(stacked, order, axis=0)
    slots, channels, width = piece.shape
    return ordered.transpose(1, 2, 0, 3).reshape(slots, channels, count * width)


def shift_right(x, amount, bits):
    for b in range(bits):
        step = 1 << b
        moved = jnp.concatenate(
            [jnp.zeros(x.shape[:-1] + (step,), x.dtype), x[..., :-step]], axis=-1
        )
        x = jnp.where(((amount >> b) & 1)[:, None, None] == 1, moved, x)
    return x


def atom_rows(projector_full, coupling, atom_start, atom_count, ext):
    slots, channels, support = projector_full.shape
    first = jnp.clip(atom_start.astype(jnp.int32), 0, ext - support)
    padded = jnp.concatenate(
        [projector_full, jnp.zeros((slots, channels, ext - support), projector_full.dtype)], axis=-1
    )
    placed = shift_right(padded, first, (ext - support).bit_length())
    live = jnp.arange(slots, dtype=jnp.int32)[:, None] < atom_count.astype(jnp.int32)[None, :]
    weights = coupling * live.astype(jnp.float32)
    return placed.reshape(slots * channels, ext), weights.reshape(slots * channels)


def cell_rows(connectivity, ext):
    cells, nodes = connectivity.shape
    rows = jnp.arange(ext, dtype=connectivity.dtype)
    onehot = (connectivity[:, :, None] == rows[None, None, :]).astype(jnp.float32)
    return onehot.reshape(cells * nodes, ext)


def scatter_rows(onehot, values):
    return lax.dot_general(
        onehot, values, (((0,), (0,)), ((), ())), precision=lax.Precision.HIGH
    )


def on_device(
    wavefunctions, cell_matrix, connectivity, projector, coupling, atom_start, atom_count
):
    own = wavefunctions.shape[0]
    g = GHOST
    ext = own + 2 * g
    count = lax.axis_size("dom")
    me = lax.axis_index("dom")

    low = from_left(wavefunctions[own - g :], "dom")
    high = from_right(wavefunctions[:g], "dom")
    extended = jnp.concatenate([low, wavefunctions, high], axis=0)

    placed, weights = atom_rows(gather_band(projector), coupling, atom_start, atom_count, ext)
    onehot = cell_rows(connectivity, ext)
    cells, nodes, _ = cell_matrix.shape
    high = lax.Precision.HIGH

    coefficients = jnp.dot(placed, extended, precision=high) * weights[:, None]
    gathered = jnp.dot(onehot, extended, precision=high).reshape(cells, nodes, -1)
    local = jnp.einsum("cij,cjb->cib", cell_matrix, gathered, precision=high)
    first = scatter_rows(onehot, local.reshape(cells * nodes, -1)) + jnp.dot(
        placed.T, coefficients, precision=high
    )

    matrices, placed_late, weights_late, first = lax.optimization_barrier(
        (cell_matrix, placed, weights, first)
    )
    moved = jnp.einsum(
        "cij,cjq->ciq", matrices, onehot.reshape(cells, nodes, ext), precision=high
    )
    operator = scatter_rows(onehot, moved.reshape(cells * nodes, ext)) + jnp.dot(
        (placed_late * weights_late[:, None]).T, placed_late, precision=highest
    )
    left_sums = from_left(first[ext - 2 * g :], "dom")
    right_sums = from_right(first[: 2 * g], "dom")
    zeros_side = jnp.zeros((ext - 2 * g, first.shape[1]), jnp.float32)
    first_image = (
        first
        + jnp.concatenate([left_sums, zeros_side], axis=0)
        + jnp.concatenate([zeros_side, right_sums], axis=0)
    )
    step_ext = (first_image - filter_center * extended) / filter_half
    row = lax.broadcasted_iota(jnp.int32, (ext, 1), 0)
    keep = jnp.logical_and(
        jnp.logical_or(row >= g, me > 0), jnp.logical_or(row < ext - g, me < count - 1)
    )
    step_ext = jnp.where(keep, step_ext, 0.0)
    step_one = step_ext[g : g + own]

    edges = jnp.concatenate([operator[:g], operator[ext - g :]], axis=0)
    second_edges = jnp.dot(edges, step_ext, precision=lax.Precision.HIGH)
    from_before = from_left(second_edges[g:], "dom")
    from_after = from_right(second_edges[:g], "dom")
    owned = lax.optimization_barrier(
        jnp.dot(operator[g : g + own], step_ext, precision=lax.Precision.HIGH)
        - filter_center * step_one
    )
    zeros_own = jnp.zeros((own - g, owned.shape[1]), jnp.float32)
    second_image = (
        owned
        + jnp.concatenate([from_before, zeros_own], axis=0)
        + jnp.concatenate([zeros_own, from_after], axis=0)
    )
    filtered = 2.0 * second_image / filter_half - wavefunctions
    return filtered


def solution(mesh):
    return jax.shard_map(
        on_device,
        mesh=mesh,
        in_specs=(
            P("dom", "band"),
            P("dom", None, None),
            P("dom", None),
            P("dom", None, "band"),
            P("dom", None),
            P("dom"),
            P("dom"),
        ),
        out_specs=P("dom", "band"),
        check_vma=False,
    )
```

```python
import jax
import jax.numpy as jnp
from jax import lax
from jax.sharding import PartitionSpec as P

GHOST = 128


filter_center = 0.25
filter_half = 2.0
highest = lax.Precision.HIGHEST


def from_left(x, axis):
    count = lax.axis_size(axis)
    return lax.ppermute(x, axis, [(i, i + 1) for i in range(count - 1)])


def from_right(x, axis):
    count = lax.axis_size(axis)
    return lax.ppermute(x, axis, [(i + 1, i) for i in range(count - 1)])


def gather_band(piece):
    count = lax.axis_size("band")
    me = lax.axis_index("band")
    pieces = [piece]
    for k in range(1, count):
        pieces.append(
            lax.ppermute(piece, "band", [(i, (i + k) % count) for i in range(count)])
        )
    stacked = jnp.stack(pieces)
    order = (me - jnp.arange(count)) % count
    ordered = jnp.take(stacked, order, axis=0)
    slots, channels, width = piece.shape
    return ordered.transpose(1, 2, 0, 3).reshape(slots, channels, count * width)


def shift_right(x, amount, bits):
    for b in range(bits):
        step = 1 << b
        moved = jnp.concatenate(
            [jnp.zeros(x.shape[:-1] + (step,), x.dtype), x[..., :-step]], axis=-1
        )
        x = jnp.where(((amount >> b) & 1)[:, None, None] == 1, moved, x)
    return x


def atom_rows(projector_full, coupling, atom_start, atom_count, ext):
    slots, channels, support = projector_full.shape
    first = jnp.clip(atom_start.astype(jnp.int32), 0, ext - support)
    padded = jnp.concatenate(
        [projector_full, jnp.zeros((slots, channels, ext - support), projector_full.dtype)], axis=-1
    )
    placed = shift_right(padded, first, (ext - support).bit_length())
    live = jnp.arange(slots, dtype=jnp.int32)[:, None] < atom_count.astype(jnp.int32)[None, :]
    weights = coupling * live.astype(jnp.float32)
    return placed.reshape(slots * channels, ext), weights.reshape(slots * channels)


def cell_rows(connectivity, ext):
    cells, nodes = connectivity.shape
    rows = jnp.arange(ext, dtype=connectivity.dtype)
    onehot = (connectivity[:, :, None] == rows[None, None, :]).astype(jnp.float32)
    return onehot.reshape(cells * nodes, ext)


def scatter_rows(onehot, values):
    return lax.dot_general(
        onehot, values, (((0,), (0,)), ((), ())), precision=lax.Precision.HIGH
    )


def on_device(
    wavefunctions, cell_matrix, connectivity, projector, coupling, atom_start, atom_count
):
    own = wavefunctions.shape[0]
    g = GHOST
    ext = own + 2 * g
    count = lax.axis_size("dom")
    me = lax.axis_index("dom")

    low = from_left(wavefunctions[own - g :], "dom")
    high = from_right(wavefunctions[:g], "dom")
    extended = jnp.concatenate([low, wavefunctions, high], axis=0)

    placed, weights = atom_rows(gather_band(projector), coupling, atom_start, atom_count, ext)
    onehot = cell_rows(connectivity, ext)
    cells, nodes, _ = cell_matrix.shape
    high = lax.Precision.HIGH

    coefficients = jnp.dot(placed, extended, precision=high) * weights[:, None]
    gathered = jnp.dot(onehot, extended, precision=high).reshape(cells, nodes, -1)
    local = jnp.einsum("cij,cjb->cib", cell_matrix, gathered, precision=high)
    local = local.reshape(cells * nodes, -1)
    scaled = placed.T
    first_outer = jnp.concatenate(
        [
            scatter_rows(onehot[:, part], local) + jnp.dot(scaled[part], coefficients, precision=high)
            for part in (slice(0, 2 * g), slice(ext - 2 * g, ext))
        ],
        axis=0,
    )
    matrices, placed_late, weights_late, local, coefficients, first_outer = (
        lax.optimization_barrier((cell_matrix, placed, weights, local, coefficients, first_outer))
    )
    middle = scatter_rows(onehot[:, 2 * g : ext - 2 * g], local) + jnp.dot(
        placed_late.T[2 * g : ext - 2 * g], coefficients, precision=high
    )
    first = jnp.concatenate([first_outer[: 2 * g], middle, first_outer[2 * g :]], axis=0)
    moved = jnp.einsum(
        "cij,cjq->ciq", matrices, onehot.reshape(cells, nodes, ext), precision=high
    )
    operator = scatter_rows(onehot, moved.reshape(cells * nodes, ext)) + jnp.dot(
        (placed_late * weights_late[:, None]).T, placed_late, precision=highest
    )
    left_sums = from_left(first_outer[2 * g :], "dom")
    right_sums = from_right(first_outer[: 2 * g], "dom")
    zeros_side = jnp.zeros((ext - 2 * g, first.shape[1]), jnp.float32)
    first_image = (
        first
        + jnp.concatenate([left_sums, zeros_side], axis=0)
        + jnp.concatenate([zeros_side, right_sums], axis=0)
    )
    step_ext = (first_image - filter_center * extended) / filter_half
    row = lax.broadcasted_iota(jnp.int32, (ext, 1), 0)
    keep = jnp.logical_and(
        jnp.logical_or(row >= g, me > 0), jnp.logical_or(row < ext - g, me < count - 1)
    )
    step_ext = jnp.where(keep, step_ext, 0.0)
    step_one = step_ext[g : g + own]

    edges = jnp.concatenate([operator[:g], operator[ext - g :]], axis=0)
    second_edges = jnp.dot(edges, step_ext, precision=lax.Precision.HIGH)
    from_before = from_left(second_edges[g:], "dom")
    from_after = from_right(second_edges[:g], "dom")
    owned = lax.optimization_barrier(
        jnp.dot(operator[g : g + own], step_ext, precision=lax.Precision.HIGH)
        - filter_center * step_one
    )
    zeros_own = jnp.zeros((own - g, owned.shape[1]), jnp.float32)
    second_image = (
        owned
        + jnp.concatenate([from_before, zeros_own], axis=0)
        + jnp.concatenate([zeros_own, from_after], axis=0)
    )
    filtered = 2.0 * second_image / filter_half - wavefunctions
    return filtered


def solution(mesh):
    return jax.shard_map(
        on_device,
        mesh=mesh,
        in_specs=(
            P("dom", "band"),
            P("dom", None, None),
            P("dom", None),
            P("dom", None, "band"),
            P("dom", None),
            P("dom"),
            P("dom"),
        ),
        out_specs=P("dom", "band"),
        check_vma=False,
    )
```

```python
import jax
import jax.numpy as jnp
from jax import lax
from jax.sharding import PartitionSpec as P

GHOST = 128


filter_center = 0.25
filter_half = 2.0
highest = lax.Precision.HIGHEST


def from_left(x, axis):
    count = lax.axis_size(axis)
    return lax.ppermute(x, axis, [(i, i + 1) for i in range(count - 1)])


def from_right(x, axis):
    count = lax.axis_size(axis)
    return lax.ppermute(x, axis, [(i + 1, i) for i in range(count - 1)])


def gather_band(piece):
    count = lax.axis_size("band")
    me = lax.axis_index("band")
    pieces = [piece]
    for k in range(1, count):
        pieces.append(
            lax.ppermute(piece, "band", [(i, (i + k) % count) for i in range(count)])
        )
    stacked = jnp.stack(pieces)
    order = (me - jnp.arange(count)) % count
    ordered = jnp.take(stacked, order, axis=0)
    slots, channels, width = piece.shape
    return ordered.transpose(1, 2, 0, 3).reshape(slots, channels, count * width)


def shift_right(x, amount, bits):
    for b in range(bits):
        step = 1 << b
        moved = jnp.concatenate(
            [jnp.zeros(x.shape[:-1] + (step,), x.dtype), x[..., :-step]], axis=-1
        )
        x = jnp.where(((amount >> b) & 1)[:, None, None] == 1, moved, x)
    return x


def atom_rows(projector_full, coupling, atom_start, atom_count, ext):
    slots, channels, support = projector_full.shape
    first = jnp.clip(atom_start.astype(jnp.int32), 0, ext - support)
    padded = jnp.concatenate(
        [projector_full, jnp.zeros((slots, channels, ext - support), projector_full.dtype)], axis=-1
    )
    placed = shift_right(padded, first, (ext - support).bit_length())
    live = jnp.arange(slots, dtype=jnp.int32)[:, None] < atom_count.astype(jnp.int32)[None, :]
    weights = coupling * live.astype(jnp.float32)
    return placed.reshape(slots * channels, ext), weights.reshape(slots * channels)


def cell_rows(connectivity, ext):
    cells, nodes = connectivity.shape
    rows = jnp.arange(ext, dtype=connectivity.dtype)
    onehot = (connectivity[:, :, None] == rows[None, None, :]).astype(jnp.float32)
    return onehot.reshape(cells * nodes, ext)


def scatter_rows(onehot, values):
    return lax.dot_general(
        onehot, values, (((0,), (0,)), ((), ())), precision=lax.Precision.HIGH
    )


def on_device(
    wavefunctions, cell_matrix, connectivity, projector, coupling, atom_start, atom_count
):
    own = wavefunctions.shape[0]
    g = GHOST
    ext = own + 2 * g
    count = lax.axis_size("dom")
    me = lax.axis_index("dom")

    low = from_left(wavefunctions[own - g :], "dom")
    high = from_right(wavefunctions[:g], "dom")
    extended = jnp.concatenate([low, wavefunctions, high], axis=0)

    placed, weights = atom_rows(gather_band(projector), coupling, atom_start, atom_count, ext)
    onehot = cell_rows(connectivity, ext)
    cells, nodes, _ = cell_matrix.shape
    high = lax.Precision.HIGH

    maps = jnp.concatenate([onehot, placed], axis=0)
    picked = jnp.dot(maps, extended, precision=high)
    gathered = picked[: cells * nodes].reshape(cells, nodes, -1)
    coefficients = picked[cells * nodes :] * weights[:, None]
    local = jnp.einsum("cij,cjb->cib", cell_matrix, gathered, precision=high)
    first = scatter_rows(
        maps, jnp.concatenate([local.reshape(cells * nodes, -1), coefficients], axis=0)
    )

    matrices, placed_late, weights_late, first = lax.optimization_barrier(
        (cell_matrix, placed, weights, first)
    )
    moved = jnp.einsum(
        "cij,cjq->ciq", matrices, onehot.reshape(cells, nodes, ext), precision=high
    )
    operator = scatter_rows(onehot, moved.reshape(cells * nodes, ext)) + jnp.dot(
        (placed_late * weights_late[:, None]).T, placed_late, precision=highest
    )
    left_sums = from_left(first[ext - 2 * g :], "dom")
    right_sums = from_right(first[: 2 * g], "dom")
    zeros_side = jnp.zeros((ext - 2 * g, first.shape[1]), jnp.float32)
    first_image = (
        first
        + jnp.concatenate([left_sums, zeros_side], axis=0)
        + jnp.concatenate([zeros_side, right_sums], axis=0)
    )
    step_ext = (first_image - filter_center * extended) / filter_half
    row = lax.broadcasted_iota(jnp.int32, (ext, 1), 0)
    keep = jnp.logical_and(
        jnp.logical_or(row >= g, me > 0), jnp.logical_or(row < ext - g, me < count - 1)
    )
    step_ext = jnp.where(keep, step_ext, 0.0)
    step_one = step_ext[g : g + own]

    edges = jnp.concatenate([operator[:g], operator[ext - g :]], axis=0)
    second_edges = jnp.dot(edges, step_ext, precision=lax.Precision.HIGH)
    from_before = from_left(second_edges[g:], "dom")
    from_after = from_right(second_edges[:g], "dom")
    owned = lax.optimization_barrier(
        jnp.dot(operator[g : g + own], step_ext, precision=lax.Precision.HIGH)
        - filter_center * step_one
    )
    zeros_own = jnp.zeros((own - g, owned.shape[1]), jnp.float32)
    second_image = (
        owned
        + jnp.concatenate([from_before, zeros_own], axis=0)
        + jnp.concatenate([zeros_own, from_after], axis=0)
    )
    filtered = 2.0 * second_image / filter_half - wavefunctions
    return filtered


def solution(mesh):
    return jax.shard_map(
        on_device,
        mesh=mesh,
        in_specs=(
            P("dom", "band"),
            P("dom", None, None),
            P("dom", None),
            P("dom", None, "band"),
            P("dom", None),
            P("dom"),
            P("dom"),
        ),
        out_specs=P("dom", "band"),
        check_vma=False,
    )
```

```python
import jax
import jax.numpy as jnp
from jax import lax
from jax.sharding import PartitionSpec as P

GHOST = 128


filter_center = 0.25
filter_half = 2.0
highest = lax.Precision.HIGHEST


def from_left(x, axis):
    count = lax.axis_size(axis)
    return lax.ppermute(x, axis, [(i, i + 1) for i in range(count - 1)])


def from_right(x, axis):
    count = lax.axis_size(axis)
    return lax.ppermute(x, axis, [(i + 1, i) for i in range(count - 1)])


def gather_band(piece):
    count = lax.axis_size("band")
    me = lax.axis_index("band")
    pieces = [piece]
    for k in range(1, count):
        pieces.append(
            lax.ppermute(piece, "band", [(i, (i + k) % count) for i in range(count)])
        )
    stacked = jnp.stack(pieces)
    order = (me - jnp.arange(count)) % count
    ordered = jnp.take(stacked, order, axis=0)
    slots, channels, width = piece.shape
    return ordered.transpose(1, 2, 0, 3).reshape(slots, channels, count * width)


def shift_right(x, amount, bits):
    for b in range(bits):
        step = 1 << b
        moved = jnp.concatenate(
            [jnp.zeros(x.shape[:-1] + (step,), x.dtype), x[..., :-step]], axis=-1
        )
        x = jnp.where(((amount >> b) & 1)[:, None, None] == 1, moved, x)
    return x


def atom_rows(projector_full, coupling, atom_start, atom_count, ext):
    slots, channels, support = projector_full.shape
    first = jnp.clip(atom_start.astype(jnp.int32), 0, ext - support)
    padded = jnp.concatenate(
        [projector_full, jnp.zeros((slots, channels, ext - support), projector_full.dtype)], axis=-1
    )
    placed = shift_right(padded, first, (ext - support).bit_length())
    live = jnp.arange(slots, dtype=jnp.int32)[:, None] < atom_count.astype(jnp.int32)[None, :]
    weights = coupling * live.astype(jnp.float32)
    return placed.reshape(slots * channels, ext), weights.reshape(slots * channels)


def cell_rows(connectivity, ext):
    cells, nodes = connectivity.shape
    rows = jnp.arange(ext, dtype=connectivity.dtype)
    onehot = (connectivity[:, :, None] == rows[None, None, :]).astype(jnp.float32)
    return onehot.reshape(cells * nodes, ext)


def scatter_rows(onehot, values):
    return lax.dot_general(
        onehot, values, (((0,), (0,)), ((), ())), precision=lax.Precision.HIGH
    )


def on_device(
    wavefunctions, cell_matrix, connectivity, projector, coupling, atom_start, atom_count
):
    own = wavefunctions.shape[0]
    g = GHOST
    ext = own + 2 * g
    count = lax.axis_size("dom")
    me = lax.axis_index("dom")

    low = from_left(wavefunctions[own - g :], "dom")
    high = from_right(wavefunctions[:g], "dom")
    extended = jnp.concatenate([low, wavefunctions, high], axis=0)

    placed, weights = atom_rows(gather_band(projector), coupling, atom_start, atom_count, ext)
    onehot = cell_rows(connectivity, ext)
    cells, nodes, _ = cell_matrix.shape
    high = lax.Precision.HIGH

    coefficients = jnp.dot(placed, extended, precision=high) * weights[:, None]
    gathered = jnp.dot(onehot, extended, precision=high).reshape(cells, nodes, -1)
    local = jnp.einsum("cij,cjb->cib", cell_matrix, gathered, precision=high)
    first = scatter_rows(onehot, local.reshape(cells * nodes, -1)) + jnp.dot(
        placed.T, coefficients, precision=high
    )

    matrices, placed_late, weights_late, first = lax.optimization_barrier(
        (cell_matrix, placed, weights, first)
    )
    moved = jnp.einsum(
        "cij,cjq->ciq", matrices, onehot.reshape(cells, nodes, ext), precision=high
    )
    operator = scatter_rows(onehot, moved.reshape(cells * nodes, ext)) + jnp.dot(
        (placed_late * weights_late[:, None]).T, placed_late, precision=highest
    )
    left_sums = from_left(first[ext - 2 * g :], "dom")
    right_sums = from_right(first[: 2 * g], "dom")
    zeros_side = jnp.zeros((ext - 2 * g, first.shape[1]), jnp.float32)
    first_image = (
        first
        + jnp.concatenate([left_sums, zeros_side], axis=0)
        + jnp.concatenate([zeros_side, right_sums], axis=0)
    )
    step_ext = (first_image - filter_center * extended) / filter_half
    row = lax.broadcasted_iota(jnp.int32, (ext, 1), 0)
    keep = jnp.logical_and(
        jnp.logical_or(row >= g, me > 0), jnp.logical_or(row < ext - g, me < count - 1)
    )
    step_ext = jnp.where(keep, step_ext, 0.0)
    step_one = step_ext[g : g + own]

    edges = jnp.concatenate([operator[:g], operator[ext - g :]], axis=0)
    second_edges = jnp.dot(edges, step_ext, precision=lax.Precision.HIGH)
    from_before = from_left(second_edges[g:], "dom")
    from_after = from_right(second_edges[:g], "dom")
    owned = lax.optimization_barrier(
        jnp.dot(operator[g : g + own], step_ext, precision=lax.Precision.HIGH)
        - filter_center * step_one
        - wavefunctions
    )
    zeros_own = jnp.zeros((own - g, owned.shape[1]), jnp.float32)
    second_image = (
        owned
        + jnp.concatenate([from_before, zeros_own], axis=0)
        + jnp.concatenate([zeros_own, from_after], axis=0)
    )
    return second_image


def solution(mesh):
    return jax.shard_map(
        on_device,
        mesh=mesh,
        in_specs=(
            P("dom", "band"),
            P("dom", None, None),
            P("dom", None),
            P("dom", None, "band"),
            P("dom", None),
            P("dom"),
            P("dom"),
        ),
        out_specs=P("dom", "band"),
        check_vma=False,
    )
```

```python
import jax
import jax.numpy as jnp
from jax import lax
from jax.sharding import PartitionSpec as P

GHOST = 128


filter_center = 0.25
filter_half = 2.0
highest = lax.Precision.HIGHEST


def from_left(x, axis):
    count = lax.axis_size(axis)
    return lax.ppermute(x, axis, [(i, i + 1) for i in range(count - 1)])


def from_right(x, axis):
    count = lax.axis_size(axis)
    return lax.ppermute(x, axis, [(i + 1, i) for i in range(count - 1)])


def gather_band(piece):
    count = lax.axis_size("band")
    me = lax.axis_index("band")
    pieces = [piece]
    for k in range(1, count):
        pieces.append(
            lax.ppermute(piece, "band", [(i, (i + k) % count) for i in range(count)])
        )
    stacked = jnp.stack(pieces)
    order = (me - jnp.arange(count)) % count
    ordered = jnp.take(stacked, order, axis=0)
    slots, channels, width = piece.shape
    return ordered.transpose(1, 2, 0, 3).reshape(slots, channels, count * width)


def shift_right(x, amount, bits):
    for b in range(bits):
        step = 1 << b
        moved = jnp.concatenate(
            [jnp.zeros(x.shape[:-1] + (step,), x.dtype), x[..., :-step]], axis=-1
        )
        x = jnp.where(((amount >> b) & 1)[:, None, None] == 1, moved, x)
    return x


def atom_rows(projector_full, coupling, atom_start, atom_count, ext):
    slots, channels, support = projector_full.shape
    first = jnp.clip(atom_start.astype(jnp.int32), 0, ext - support)
    padded = jnp.concatenate(
        [projector_full, jnp.zeros((slots, channels, ext - support), projector_full.dtype)], axis=-1
    )
    placed = shift_right(padded, first, (ext - support).bit_length())
    live = jnp.arange(slots, dtype=jnp.int32)[:, None] < atom_count.astype(jnp.int32)[None, :]
    weights = coupling * live.astype(jnp.float32)
    return placed.reshape(slots * channels, ext), weights.reshape(slots * channels)


def cell_rows(connectivity, ext):
    cells, nodes = connectivity.shape
    rows = jnp.arange(ext, dtype=connectivity.dtype)
    onehot = (connectivity[:, :, None] == rows[None, None, :]).astype(jnp.float32)
    return onehot.reshape(cells * nodes, ext)


def scatter_rows(onehot, values):
    return lax.dot_general(
        onehot, values, (((0,), (0,)), ((), ())), precision=lax.Precision.HIGH
    )


def on_device(
    wavefunctions, cell_matrix, connectivity, projector, coupling, atom_start, atom_count
):
    own = wavefunctions.shape[0]
    g = GHOST
    ext = own + 2 * g
    count = lax.axis_size("dom")
    me = lax.axis_index("dom")

    low = from_left(wavefunctions[own - g :], "dom")
    high = from_right(wavefunctions[:g], "dom")
    extended = jnp.concatenate([low, wavefunctions, high], axis=0)

    placed, weights = atom_rows(gather_band(projector), coupling, atom_start, atom_count, ext)
    onehot = cell_rows(connectivity, ext)
    cells, nodes, _ = cell_matrix.shape
    high = lax.Precision.HIGH

    coefficients = jnp.dot(placed, extended, precision=high) * weights[:, None]
    gathered = jnp.dot(onehot, extended, precision=high).reshape(cells, nodes, -1)
    local = jnp.einsum("cij,cjb->cib", cell_matrix, gathered, precision=high)
    first = scatter_rows(onehot, local.reshape(cells * nodes, -1)) + jnp.dot(
        placed.T, coefficients, precision=high
    )

    matrices, placed_late, weights_late, first = lax.optimization_barrier(
        (cell_matrix, placed, weights, first)
    )
    moved = jnp.einsum(
        "cij,cjq->ciq", matrices, onehot.reshape(cells, nodes, ext), precision=high
    )
    operator = scatter_rows(onehot, moved.reshape(cells * nodes, ext)) + jnp.dot(
        (placed_late * weights_late[:, None]).T, placed_late, precision=highest
    )
    left_sums = from_left(first[ext - 2 * g :], "dom")
    right_sums = from_right(first[: 2 * g], "dom")
    zeros_side = jnp.zeros((ext - 2 * g, first.shape[1]), jnp.float32)
    (pending,) = lax.optimization_barrier((first - filter_center * extended,))
    step_ext = (
        pending
        + jnp.concatenate([left_sums, zeros_side], axis=0)
        + jnp.concatenate([zeros_side, right_sums], axis=0)
    ) / filter_half
    row = lax.broadcasted_iota(jnp.int32, (ext, 1), 0)
    keep = jnp.logical_and(
        jnp.logical_or(row >= g, me > 0), jnp.logical_or(row < ext - g, me < count - 1)
    )
    step_ext = jnp.where(keep, step_ext, 0.0)
    step_one = step_ext[g : g + own]

    edges = jnp.concatenate([operator[:g], operator[ext - g :]], axis=0)
    second_edges = jnp.dot(edges, step_ext, precision=lax.Precision.HIGH)
    from_before = from_left(second_edges[g:], "dom")
    from_after = from_right(second_edges[:g], "dom")
    owned = lax.optimization_barrier(
        jnp.dot(operator[g : g + own], step_ext, precision=lax.Precision.HIGH)
        - filter_center * step_one
        - wavefunctions
    )
    zeros_own = jnp.zeros((own - g, owned.shape[1]), jnp.float32)
    second_image = (
        owned
        + jnp.concatenate([from_before, zeros_own], axis=0)
        + jnp.concatenate([zeros_own, from_after], axis=0)
    )
    return second_image


def solution(mesh):
    return jax.shard_map(
        on_device,
        mesh=mesh,
        in_specs=(
            P("dom", "band"),
            P("dom", None, None),
            P("dom", None),
            P("dom", None, "band"),
            P("dom", None),
            P("dom"),
            P("dom"),
        ),
        out_specs=P("dom", "band"),
        check_vma=False,
    )
```
